256 devices in a mesh: head: 8 (over z), ctx: 32 (over y, x, core).
Axes of the slice: x: 4, y: 4, z: 8, core: 2. Of those that a mesh axis runs over, the one named last changes fastest.
Arguments:
- queries: bfloat16 [16384, 4096], P('ctx', 'head'), may hold values from -6 to 6
- key_head_tensor: bfloat16 [16384, 2048], P('ctx', 'head'), may hold values from -6 to 6
- value_head_tensor: bfloat16 [16384, 2048], P('ctx', 'head'), may hold values from -6 to 6
- output_gradient: bfloat16 [16384, 4096], P('ctx', 'head'), may hold values from -6 to 6
- adapter_up_matrix: bfloat16 [16, 4096], P(None, 'head'), may hold values from -0.09375 to 0.09375
- document_block_counts: int32 [32], replicated, may hold values from 1 to 32, 128 in all
Outputs:
- attention_output: bfloat16 [16384, 4096], P('ctx', 'head')
- query_gradient: bfloat16 [16384, 4096], P('ctx', 'head')
- key_gradient: bfloat16 [16384, 2048], P('ctx', 'head')
- value_gradient: bfloat16 [16384, 2048], P('ctx', 'head')
- adapter_gradient: float32 [16384, 16], P('ctx')
The draws below stay inside these ranges and needn't reach their ends.
Inputs may be any that keep to these rules, and one draw needn't show every extreme that they name: Document i holds document_block_counts[i] * 128 consecutive tokens; the documents fill all 128 blocks in order.
All inputs are finite; a program needn't handle non-finite values.
Results may differ from the reference program's by a relative error of at most 0.012.
Values may be sent and summed in bfloat16 or wider, within the bound.
No kernel may reach another device: no remote copies, remote signals or barrier semaphores. Data moves between devices by JAX's collectives and lax.ppermute only.
A program may use at most 128 MiB of HBM per device.

```python
import math
import jax
import jax.numpy as jnp
import numpy as np
from jax import lax

HEAD_SIZE = 128
QUERY_HEADS = 32
KVH = 16
WIN = 1024
ADAPTER_RANK = 16
BLK = 128
TOKENS = 16384
NBLK = 128
DOCS = 32
DOC_MOST = 32


def draw_queries(key, part):
    noise_key = jax.random.fold_in(jax.random.fold_in(key, 11), 0)
    values = jnp.clip(jax.random.normal(noise_key, (TOKENS, QUERY_HEADS * HEAD_SIZE), jnp.float32) * 1.5, -6.0, 6.0)
    return values.astype(jnp.bfloat16)


def draw_key_head_tensor(key, part):
    noise_key = jax.random.fold_in(jax.random.fold_in(key, 23), 0)
    values = jnp.clip(jax.random.normal(noise_key, (TOKENS, KVH * HEAD_SIZE), jnp.float32) * 1.5, -6.0, 6.0)
    return values.astype(jnp.bfloat16)


def level_of(key, dims, cuts, least, high):
    level = 1.0
    for axis_at, shards_of in cuts:
        draws = jax.random.uniform(jax.random.fold_in(jax.random.fold_in(key, 6), axis_at), (shards_of,), jnp.float32, least / len(cuts), high / len(cuts))
        level = level * jnp.repeat(jnp.exp(draws), dims[axis_at] // shards_of).reshape((-1,) + (1,) * (len(dims) - 1 - axis_at))
    return level


def length_profile(number_of, total, limit, lean):
    portions = [(1 << 20) // math.isqrt(rank ** lean) + 1 for rank in range(2, number_of + 1)]
    surplus, counts = total - limit - (number_of - 1), [1] * (number_of - 1)
    while surplus > 0:
        free = [i for i in range(number_of - 1) if counts[i] < limit]
        whole, remaining = sum([portions[i] for i in free]), surplus
        for i in free:
            extra = min(limit - counts[i], max(1, remaining * portions[i] // whole), surplus)
            counts[i] = counts[i] + extra
            surplus = surplus - extra
    return np.array([limit] + counts)


def uneven(own_key, count, total, limit, skew):
    if count == 2:
        one = jax.random.randint(own_key, (), max(1, total - limit), min(limit, total - 1) + 1)
        return jnp.stack([one, total - one])
    lengths = jnp.asarray(length_profile(count, total, limit, skew), jnp.int32)
    twos = (count - 1) // 2
    donor, taker = lengths[1:1 + 2 * twos:2], lengths[2:2 + 2 * twos:2]
    slack = jnp.minimum(donor - 1, limit - taker)
    moved = jax.random.randint(jax.random.fold_in(own_key, 1), (twos,), 0, 1 << 20) % (slack + 1)
    lengths = lengths.at[1:1 + 2 * twos:2].set(donor - moved).at[2:2 + 2 * twos:2].set(taker + moved)
    return lengths[jax.random.permutation(jax.random.fold_in(own_key, 2), count)]


def normal_values(key, dims, scale, limit, cuts=(), kind=jnp.bfloat16):
    loudness = level_of(key, dims, cuts, -0.22, 0.18) if cuts else 1.0
    drawn = jax.random.normal(key, dims, jnp.float32) * scale * loudness
    return jnp.minimum(jnp.maximum(drawn, -limit), limit).astype(kind)


def setup_inputs(seed: int = 0) -> dict:
    splits = jax.random.split(jax.random.key(seed), 7)
    return {
        "queries": draw_queries(jax.random.fold_in(splits[6], 71), 0),
        "key_head_tensor": draw_key_head_tensor(jax.random.fold_in(splits[6], 71), 0),
        "value_head_tensor": normal_values(splits[2], (TOKENS, KVH * HEAD_SIZE), 1.0, 6.0, ((0, 32), (1, 8))),
        "output_gradient": normal_values(splits[3], (TOKENS, QUERY_HEADS * HEAD_SIZE), 1.0, 6.0, ((0, 32), (1, 8))),
        "adapter_up_matrix": normal_values(splits[4], (ADAPTER_RANK, QUERY_HEADS * HEAD_SIZE), (QUERY_HEADS * HEAD_SIZE) ** -0.5, 0.09375, ((1, 8),)),
        "document_block_counts": uneven(splits[5], DOCS, NBLK, DOC_MOST, 2).astype(jnp.int32),
    }


softmax_scale = 168.0 ** -0.5
masked_value = -1.0e30


def reference(queries, key_head_tensor, value_head_tensor, output_gradient, adapter_up_matrix, document_block_counts):
    doc_ends = jnp.cumsum(document_block_counts).astype(jnp.int32) * BLK
    positions = jnp.arange(TOKENS, dtype=jnp.int32)
    documents = jnp.sum((positions[:, None] >= doc_ends[None, :]).astype(jnp.int32), axis=1)
    pad_docs = jnp.concatenate([jnp.full((WIN,), -1, jnp.int32), documents])
    query_heads = queries.reshape(TOKENS, KVH, 2, HEAD_SIZE)
    grad_heads = output_gradient.reshape(TOKENS, KVH, 2, HEAD_SIZE)
    pad_keys = jnp.concatenate([jnp.zeros((WIN, KVH, HEAD_SIZE), key_head_tensor.dtype), key_head_tensor.reshape(TOKENS, KVH, HEAD_SIZE)])
    pad_values = jnp.concatenate([jnp.zeros((WIN, KVH, HEAD_SIZE), value_head_tensor.dtype), value_head_tensor.reshape(TOKENS, KVH, HEAD_SIZE)])
    key_span = WIN + BLK

    def block_step(buffers, block_num):
        key_acc, value_acc = buffers
        row_start = block_num * BLK
        query_tile = lax.dynamic_slice_in_dim(query_heads, row_start, BLK, 0).astype(jnp.float32)
        grad_tile = lax.dynamic_slice_in_dim(grad_heads, row_start, BLK, 0).astype(jnp.float32)
        key_tile = lax.dynamic_slice_in_dim(pad_keys, row_start, key_span, 0).astype(jnp.float32)
        value_tile = lax.dynamic_slice_in_dim(pad_values, row_start, key_span, 0).astype(jnp.float32)
        query_docs = lax.dynamic_slice_in_dim(documents, row_start, BLK, 0)
        key_docs = lax.dynamic_slice_in_dim(pad_docs, row_start, key_span, 0)
        row_pos = row_start + jnp.arange(BLK, dtype=jnp.int32)
        col_pos = row_start - WIN + jnp.arange(key_span, dtype=jnp.int32)
        offsets = row_pos[:, None] - col_pos[None, :]
        allowed = (query_docs[:, None] == key_docs[None, :]) & (offsets >= 0) & (offsets < WIN)
        scores = jnp.einsum("iged,jgd->geij", query_tile, key_tile) * softmax_scale
        masked = jnp.where(allowed, scores, masked_value)
        row_max = jnp.max(masked, axis=-1, keepdims=True)
        row_sum = jnp.sum(jnp.where(allowed, jnp.exp(masked - row_max), 0.0), axis=-1, keepdims=True)
        log_norm = row_max + jnp.log(row_sum)
        weights = jnp.where(allowed, jnp.exp(scores - log_norm), 0.0)
        weights_low = lax.optimization_barrier(weights.astype(jnp.bfloat16)).astype(jnp.float32)
        attended = jnp.einsum("geij,jgd->iged", weights_low, value_tile)
        row_dot = jnp.transpose(jnp.sum(grad_tile * attended, axis=-1), (1, 2, 0))
        weight_grad = jnp.einsum("iged,jgd->geij", grad_tile, value_tile)
        score_grad = weights * (weight_grad - row_dot[..., None])
        score_low = lax.optimization_barrier(score_grad.astype(jnp.bfloat16)).astype(jnp.float32)
        query_grad = softmax_scale * jnp.einsum("geij,jgd->iged", score_low, key_tile)
        key_part = softmax_scale * jnp.einsum("geij,iged->jgd", score_low, query_tile)
        value_part = jnp.einsum("geij,iged->jgd", weights_low, grad_tile)
        key_acc = lax.dynamic_update_slice_in_dim(key_acc, lax.dynamic_slice_in_dim(key_acc, row_start, key_span, 0) + key_part, row_start, 0)
        value_acc = lax.dynamic_update_slice_in_dim(value_acc, lax.dynamic_slice_in_dim(value_acc, row_start, key_span, 0) + value_part, row_start, 0)
        return (key_acc, value_acc), (attended.astype(jnp.bfloat16), query_grad.astype(jnp.bfloat16))

    start_bufs = (jnp.zeros((TOKENS + WIN, KVH, HEAD_SIZE), jnp.float32), jnp.zeros((TOKENS + WIN, KVH, HEAD_SIZE), jnp.float32))
    (key_acc, value_acc), (attended_all, query_all) = lax.scan(block_step, start_bufs, jnp.arange(NBLK, dtype=jnp.int32))
    attention_output = attended_all.reshape(TOKENS, QUERY_HEADS * HEAD_SIZE)
    query_gradient = query_all.reshape(TOKENS, QUERY_HEADS * HEAD_SIZE)
    key_gradient = key_acc[WIN:].reshape(TOKENS, KVH * HEAD_SIZE).astype(jnp.bfloat16)
    value_gradient = value_acc[WIN:].reshape(TOKENS, KVH * HEAD_SIZE).astype(jnp.bfloat16)
    adapter_gradient = jnp.dot(query_gradient, jnp.transpose(adapter_up_matrix), preferred_element_type=jnp.float32)
    return attention_output, query_gradient, key_gradient, value_gradient, adapter_gradient
```

```python
import jax
import jax.numpy as jnp
from jax import lax
from jax.sharding import PartitionSpec as P

HEAD_SIZE = 128
WIN = 1024
BLK = 128


softmax_scale = 168.0 ** (-0.5)
masked_value = -1e30


def passed_along(block, axis, distance):
    devices = range(lax.axis_size(axis))
    route = [(i - distance, i) for i in devices if i - distance in devices]
    return lax.ppermute(block, axis, route)


def gathered_sum(part, axis):
    count = lax.axis_size(axis)
    received = [part]
    for shift in range(1, count):
        route = [(i, (i + shift) % count) for i in range(count)]
        received.append(lax.ppermute(part, axis, route))
    stacked = jnp.stack(received).astype(jnp.float32)
    order = (lax.axis_index(axis) - jnp.arange(count, dtype=jnp.int32)) % count
    in_order = jnp.take(stacked, order, axis=0)
    total = in_order[0]
    for j in range(1, count):
        total = total + in_order[j]
    return total


def doc_index(positions, doc_ends):
    counted = jnp.sum((positions[:, None] >= doc_ends[None, :]).astype(jnp.int32), axis=1)
    return jnp.where(positions < 0, -1, counted)


def span_scores(query_tile, key_span, query_pos, key_pos, doc_ends):
    scores = (
        jnp.einsum("iged,jgd->geij", query_tile, key_span, preferred_element_type=jnp.float32)
        * softmax_scale
    )
    row_pos = query_pos + jnp.arange(query_tile.shape[0], dtype=jnp.int32)
    col_pos = key_pos + jnp.arange(key_span.shape[0], dtype=jnp.int32)
    offsets = row_pos[:, None] - col_pos[None, :]
    same_doc = doc_index(row_pos, doc_ends)[:, None] == doc_index(col_pos, doc_ends)[None, :]
    allowed = same_doc & (offsets >= 0) & (offsets < WIN)
    return (scores, allowed)


def attend_span(query_tile, grad_tile, key_span, value_span, query_pos, key_pos, doc_ends):
    scores, allowed = span_scores(query_tile, key_span, query_pos, key_pos, doc_ends)
    attended = None
    masked = jnp.where(allowed, scores, masked_value)
    row_max = jnp.max(masked, axis=-1)
    row_sum = jnp.sum(jnp.where(allowed, jnp.exp(masked - row_max[..., None]), 0.0), axis=-1)
    log_norm = row_max + jnp.log(row_sum)
    weights = jnp.where(allowed, jnp.exp(scores - log_norm[..., None]), 0.0)
    weights_low = weights.astype(jnp.bfloat16)
    attended = jnp.einsum(
        "geij,jgd->iged", weights_low, value_span, preferred_element_type=jnp.float32
    )
    row_dot = jnp.transpose(jnp.sum(grad_tile.astype(jnp.float32) * attended, axis=-1), (1, 2, 0))
    weight_grad = jnp.einsum(
        "iged,jgd->geij", grad_tile, value_span, preferred_element_type=jnp.float32
    )
    score_grad = (weights * (weight_grad - row_dot[..., None])).astype(jnp.bfloat16)
    key_part = softmax_scale * jnp.einsum(
        "geij,iged->jgd", score_grad, query_tile, preferred_element_type=jnp.float32
    )
    value_part = jnp.einsum(
        "geij,iged->jgd", weights_low, grad_tile, preferred_element_type=jnp.float32
    )
    return (attended, score_grad, log_norm, row_dot, key_part, value_part)


def add_rows(total, part):
    return total + part


def body(
    queries,
    key_head_tensor,
    value_head_tensor,
    output_gradient,
    adapter_up_matrix,
    document_block_counts,
):
    tokens_here = queries.shape[0]
    query_cols = queries.shape[1]
    key_cols = key_head_tensor.shape[1]
    group_count = key_cols // HEAD_SIZE
    edge_rows = min(WIN, tokens_here)
    hop_count = WIN // edge_rows
    block_rows = min(tokens_here, 512)
    blocks = tokens_here // block_rows
    first_pos = lax.axis_index("ctx") * tokens_here
    lowest = first_pos - WIN
    doc_ends = jnp.cumsum(document_block_counts) * BLK
    joined = jnp.concatenate([key_head_tensor, value_head_tensor], axis=1)
    arrived = []
    for hop_num in range(hop_count):
        arrived.append(passed_along(joined, "ctx", hop_num + 1))
    extended = jnp.concatenate(arrived[::-1] + [joined], axis=0)
    ext_keys = extended[:, :key_cols].reshape(WIN + tokens_here, group_count, HEAD_SIZE)
    ext_values = extended[:, key_cols:].reshape(WIN + tokens_here, group_count, HEAD_SIZE)
    query_heads = queries.reshape(tokens_here, group_count, 2, HEAD_SIZE)
    grad_heads = output_gradient.reshape(tokens_here, group_count, 2, HEAD_SIZE)

    def one_block(block_num, buffers):
        out_buf, query_buf, key_acc, value_acc, norm_buf, dot_buf = buffers
        row_first = block_num * block_rows
        attended, score_grad, log_norm, row_dot, key_part, value_part = attend_span(
            query_heads,
            grad_heads,
            ext_keys,
            ext_values,
            first_pos + row_first,
            lowest + row_first,
            doc_ends,
        )
        query_grad = softmax_scale * jnp.einsum(
            "geij,jgd->iged", score_grad, ext_keys, preferred_element_type=jnp.float32
        )
        key_acc = add_rows(key_acc, key_part)
        value_acc = add_rows(value_acc, value_part)
        out_buf = attended.astype(jnp.bfloat16)
        query_buf = query_grad.astype(jnp.bfloat16)
        norm_buf = log_norm.reshape(2 * group_count, block_rows)
        dot_buf = row_dot.reshape(2 * group_count, block_rows)
        return (out_buf, query_buf, key_acc, value_acc, norm_buf, dot_buf)

    start_bufs = (
        jnp.zeros((tokens_here, group_count, 2, HEAD_SIZE), jnp.bfloat16),
        jnp.zeros((tokens_here, group_count, 2, HEAD_SIZE), jnp.bfloat16),
        jnp.zeros((WIN + tokens_here, group_count, HEAD_SIZE), jnp.float32),
        jnp.zeros((WIN + tokens_here, group_count, HEAD_SIZE), jnp.float32),
        jnp.zeros((2 * group_count, tokens_here), jnp.float32),
        jnp.zeros((2 * group_count, tokens_here), jnp.float32),
    )
    out_buf, query_buf, key_acc, value_acc, norm_buf, dot_buf = lax.fori_loop(
        0, blocks, one_block, start_bufs
    )
    halo_grads = jnp.concatenate(
        [key_acc[:WIN].reshape(WIN, key_cols), value_acc[:WIN].reshape(WIN, key_cols)], axis=1
    )
    returned = jnp.zeros((edge_rows, 2 * key_cols), jnp.float32)
    for hop_num in range(hop_count):
        segment = halo_grads[
            (hop_count - 1 - hop_num) * edge_rows : (hop_count - hop_num) * edge_rows
        ]
        returned = returned + passed_along(
            segment.astype(jnp.bfloat16), "ctx", -(hop_num + 1)
        ).astype(segment.dtype)
    key_total = key_acc[WIN:].reshape(tokens_here, key_cols)
    value_total = value_acc[WIN:].reshape(tokens_here, key_cols)
    cut_row = tokens_here - edge_rows
    key_total = jnp.concatenate([key_total[:cut_row], key_total + returned[:, :key_cols]], axis=0)
    value_total = jnp.concatenate(
        [value_total[:cut_row], value_total + returned[:, key_cols:]], axis=0
    )
    flattened_query = query_buf.reshape(tokens_here, query_cols)
    adapter_portion = lax.dot_general(
        flattened_query,
        adapter_up_matrix,
        (((1,), (1,)), ((), ())),
        preferred_element_type=jnp.float32,
    )
    adapter_gradient = gathered_sum(adapter_portion.astype(jnp.bfloat16), "head")
    return (
        out_buf.reshape(tokens_here, query_cols),
        flattened_query,
        key_total.astype(jnp.bfloat16),
        value_total.astype(jnp.bfloat16),
        adapter_gradient,
    )


def solution(mesh):
    in_specs = (
        P("ctx", "head"),
        P("ctx", "head"),
        P("ctx", "head"),
        P("ctx", "head"),
        P(None, "head"),
        P(),
    )
    out_specs = (
        P("ctx", "head"),
        P("ctx", "head"),
        P("ctx", "head"),
        P("ctx", "head"),
        P("ctx", None),
    )
    return jax.shard_map(body, mesh=mesh, in_specs=in_specs, out_specs=out_specs, check_vma=False)
```

```python
import jax
import jax.numpy as jnp
from jax import lax
from jax.experimental import pallas as pl
from jax.experimental.pallas import tpu as pltpu
from jax.sharding import PartitionSpec as P

HEAD_SIZE = 128
WIN = 1024
BLK = 128


softmax_scale = 168.0 ** (-0.5)
masked_value = -1e30


def passed_along(block, axis, distance):
    devices = range(lax.axis_size(axis))
    route = [(i - distance, i) for i in devices if i - distance in devices]
    return lax.ppermute(block, axis, route)


def gathered_sum(part, axis):
    count = lax.axis_size(axis)
    received = [part]
    for shift in range(1, count):
        route = [(i, (i + shift) % count) for i in range(count)]
        received.append(lax.ppermute(part, axis, route))
    stacked = jnp.stack(received).astype(jnp.float32)
    order = (lax.axis_index(axis) - jnp.arange(count, dtype=jnp.int32)) % count
    in_order = jnp.take(stacked, order, axis=0)
    total = in_order[0]
    for j in range(1, count):
        total = total + in_order[j]
    return total


def doc_index(positions, doc_ends):
    counted = jnp.sum((positions[:, None] >= doc_ends[None, :]).astype(jnp.int32), axis=1)
    return jnp.where(positions < 0, -1, counted)


def attention_kernel(q_ref, k_ref, v_ref, do_ref, qdoc_ref, kdoc_ref,
                     o_ref, dq_ref, dk_ref, dv_ref):
    qb = pl.program_id(1)
    rows = q_ref.shape[0]
    span = rows + WIN
    key_first = pl.multiple_of(qb * rows, rows)

    @pl.when(qb == 0)
    def _():
        dk_ref[...] = jnp.zeros_like(dk_ref)
        dv_ref[...] = jnp.zeros_like(dv_ref)

    q = jnp.concatenate([q_ref[:, :HEAD_SIZE], q_ref[:, HEAD_SIZE:]], axis=0)
    do = jnp.concatenate([do_ref[:, :HEAD_SIZE], do_ref[:, HEAD_SIZE:]], axis=0)
    k = k_ref[pl.ds(key_first, span), :]
    v = v_ref[pl.ds(key_first, span), :]
    qdoc = qdoc_ref[...]
    qdoc = jnp.concatenate([qdoc, qdoc], axis=0)
    kdoc = kdoc_ref[:, pl.ds(key_first, span)]
    row = lax.broadcasted_iota(jnp.int32, (2 * rows, span), 0) % rows
    col = lax.broadcasted_iota(jnp.int32, (2 * rows, span), 1)
    offset = row + WIN - col
    live = (offset >= 0) & (offset < WIN) & (qdoc == kdoc)

    s = lax.dot_general(q, k, (((1,), (1,)), ((), ())),
                        preferred_element_type=jnp.float32) * softmax_scale
    masked = jnp.where(live, s, masked_value)
    row_max = jnp.max(masked, axis=1, keepdims=True)
    e = jnp.exp(masked - row_max)
    row_sum = jnp.sum(e, axis=1, keepdims=True)
    p = e * (1.0 / row_sum)
    p_low = p.astype(jnp.bfloat16)
    o = jnp.dot(p_low, v, preferred_element_type=jnp.float32)
    row_dot = jnp.sum(do.astype(jnp.float32) * o, axis=1, keepdims=True)
    dp = lax.dot_general(do, v, (((1,), (1,)), ((), ())),
                         preferred_element_type=jnp.float32)
    ds = (p * (dp - row_dot)).astype(jnp.bfloat16)
    dq = jnp.dot(ds, k, preferred_element_type=jnp.float32) * softmax_scale
    dk = lax.dot_general(ds, q, (((0,), (0,)), ((), ())),
                         preferred_element_type=jnp.float32) * softmax_scale
    dv = lax.dot_general(p_low, do, (((0,), (0,)), ((), ())),
                         preferred_element_type=jnp.float32)
    o_ref[:, :HEAD_SIZE] = o[:rows].astype(o_ref.dtype)
    o_ref[:, HEAD_SIZE:] = o[rows:].astype(o_ref.dtype)
    dq_ref[:, :HEAD_SIZE] = dq[:rows].astype(dq_ref.dtype)
    dq_ref[:, HEAD_SIZE:] = dq[rows:].astype(dq_ref.dtype)
    dk_ref[pl.ds(key_first, span), :] += dk
    dv_ref[pl.ds(key_first, span), :] += dv


def fused_attention(queries, extended, output_gradient, qdoc, kdoc, rows=BLK):
    tokens, query_cols = queries.shape
    ext_rows, joined_cols = extended.shape
    groups = joined_cols // (2 * HEAD_SIZE)
    blocks = tokens // rows
    span = rows + WIN
    pair = 2 * HEAD_SIZE
    flops = groups * blocks * 6 * 2 * (2 * rows) * span * HEAD_SIZE
    nbytes = 2 * (4 * tokens * query_cols + ext_rows * joined_cols) + 4 * ext_rows * joined_cols
    return pl.pallas_call(
        attention_kernel,
        grid=(groups, blocks),
        in_specs=[
            pl.BlockSpec((rows, pair), lambda g, b: (b, g)),
            pl.BlockSpec((ext_rows, HEAD_SIZE), lambda g, b: (0, g)),
            pl.BlockSpec((ext_rows, HEAD_SIZE), lambda g, b: (0, g + groups)),
            pl.BlockSpec((rows, pair), lambda g, b: (b, g)),
            pl.BlockSpec((rows, 1), lambda g, b: (b, 0)),
            pl.BlockSpec((1, ext_rows), lambda g, b: (0, 0)),
        ],
        out_specs=[
            pl.BlockSpec((rows, pair), lambda g, b: (b, g)),
            pl.BlockSpec((rows, pair), lambda g, b: (b, g)),
            pl.BlockSpec((ext_rows, HEAD_SIZE), lambda g, b: (0, g)),
            pl.BlockSpec((ext_rows, HEAD_SIZE), lambda g, b: (0, g)),
        ],
        out_shape=[
            jax.ShapeDtypeStruct((tokens, query_cols), jnp.bfloat16),
            jax.ShapeDtypeStruct((tokens, query_cols), jnp.bfloat16),
            jax.ShapeDtypeStruct((ext_rows, joined_cols // 2), jnp.float32),
            jax.ShapeDtypeStruct((ext_rows, joined_cols // 2), jnp.float32),
        ],
        compiler_params=pltpu.CompilerParams(
            dimension_semantics=("arbitrary", "arbitrary"),
            vmem_limit_bytes=48 * 1024 * 1024,
        ),
        cost_estimate=pl.CostEstimate(
            flops=flops, transcendentals=groups * blocks * 2 * rows * span,
            bytes_accessed=nbytes),
    )(queries, extended, extended, output_gradient, qdoc, kdoc)


def body(
    queries,
    key_head_tensor,
    value_head_tensor,
    output_gradient,
    adapter_up_matrix,
    document_block_counts,
):
    tokens_here = queries.shape[0]
    query_cols = queries.shape[1]
    key_cols = key_head_tensor.shape[1]
    edge_rows = min(WIN, tokens_here)
    hop_count = WIN // edge_rows
    first_pos = lax.axis_index("ctx") * tokens_here
    lowest = first_pos - WIN
    doc_ends = jnp.cumsum(document_block_counts) * BLK
    joined = jnp.concatenate([key_head_tensor, value_head_tensor], axis=1)
    arrived = []
    for hop_num in range(hop_count):
        arrived.append(passed_along(joined, "ctx", hop_num + 1))
    extended = jnp.concatenate(arrived[::-1] + [joined], axis=0)
    qdoc = doc_index(first_pos + jnp.arange(tokens_here, dtype=jnp.int32), doc_ends)
    kdoc = doc_index(lowest + jnp.arange(WIN + tokens_here, dtype=jnp.int32), doc_ends)
    attended, flattened_query, key_grads, value_grads = fused_attention(
        queries, extended, output_gradient, qdoc[:, None], kdoc[None, :]
    )
    halo_grads = jnp.concatenate([key_grads[:WIN], value_grads[:WIN]], axis=1)
    returned = jnp.zeros((edge_rows, 2 * key_cols), jnp.float32)
    for hop_num in range(hop_count):
        segment = halo_grads[
            (hop_count - 1 - hop_num) * edge_rows : (hop_count - hop_num) * edge_rows
        ]
        returned = returned + passed_along(
            segment.astype(jnp.bfloat16), "ctx", -(hop_num + 1)
        ).astype(segment.dtype)
    cut_row = tokens_here - edge_rows
    own = jnp.concatenate([key_grads[WIN:], value_grads[WIN:]], axis=1)
    total = jnp.concatenate([own[:cut_row], own[cut_row:] + returned], axis=0)
    key_total = total[:, :key_cols]
    value_total = total[:, key_cols:]
    adapter_portion = lax.dot_general(
        flattened_query,
        adapter_up_matrix,
        (((1,), (1,)), ((), ())),
        preferred_element_type=jnp.float32,
    )
    adapter_gradient = gathered_sum(adapter_portion.astype(jnp.bfloat16), "head")
    return (
        attended,
        flattened_query,
        key_total.astype(jnp.bfloat16),
        value_total.astype(jnp.bfloat16),
        adapter_gradient,
    )


def solution(mesh):
    in_specs = (
        P("ctx", "head"),
        P("ctx", "head"),
        P("ctx", "head"),
        P("ctx", "head"),
        P(None, "head"),
        P(),
    )
    out_specs = (
        P("ctx", "head"),
        P("ctx", "head"),
        P("ctx", "head"),
        P("ctx", "head"),
        P("ctx", None),
    )
    return jax.shard_map(body, mesh=mesh, in_specs=in_specs, out_specs=out_specs, check_vma=False)
```

```python
import jax
import jax.numpy as jnp
from jax import lax
from jax.experimental import pallas as pl
from jax.experimental.pallas import tpu as pltpu
from jax.sharding import PartitionSpec as P

HEAD_SIZE = 128
WIN = 1024
BLK = 128


softmax_scale = 168.0 ** (-0.5)
masked_value = -1e30


def passed_along(block, axis, distance):
    devices = range(lax.axis_size(axis))
    route = [(i - distance, i) for i in devices if i - distance in devices]
    return lax.ppermute(block, axis, route)


def gathered_sum(part, axis):
    count = lax.axis_size(axis)
    total = part.astype(jnp.float32)
    stride = 1
    while stride < count:
        route = [(i, i ^ stride) for i in range(count)]
        total = total + lax.ppermute(total, axis, route)
        stride *= 2
    return total


def doc_index(positions, doc_ends):
    counted = jnp.sum((positions[:, None] >= doc_ends[None, :]).astype(jnp.int32), axis=1)
    return jnp.where(positions < 0, -1, counted)


def attention_kernel(q_ref, k_ref, v_ref, do_ref, qdoc_ref, kdoc_ref,
                     o_ref, dq_ref, dk_ref, dv_ref):
    qb = pl.program_id(1)
    rows = q_ref.shape[0]
    span = rows + WIN
    key_first = pl.multiple_of(qb * rows, rows)

    @pl.when(qb == 0)
    def _():
        dk_ref[...] = jnp.zeros_like(dk_ref)
        dv_ref[...] = jnp.zeros_like(dv_ref)

    q = jnp.concatenate([q_ref[:, :HEAD_SIZE], q_ref[:, HEAD_SIZE:]], axis=0)
    do = jnp.concatenate([do_ref[:, :HEAD_SIZE], do_ref[:, HEAD_SIZE:]], axis=0)
    k = k_ref[pl.ds(key_first, span), :]
    v = v_ref[pl.ds(key_first, span), :]
    qdoc = qdoc_ref[...]
    qdoc = jnp.concatenate([qdoc, qdoc], axis=0)
    kdoc = kdoc_ref[:, pl.ds(key_first, span)]
    row = lax.broadcasted_iota(jnp.int32, (2 * rows, span), 0) % rows
    col = lax.broadcasted_iota(jnp.int32, (2 * rows, span), 1)
    offset = row + WIN - col
    live = (offset >= 0) & (offset < WIN) & (qdoc == kdoc)

    s = lax.dot_general(q, k, (((1,), (1,)), ((), ())),
                        preferred_element_type=jnp.float32) * softmax_scale
    masked = jnp.where(live, s, masked_value)
    row_max = jnp.max(masked, axis=1, keepdims=True)
    e = jnp.exp(masked - row_max)
    row_sum = jnp.sum(e, axis=1, keepdims=True)
    p = e * (1.0 / row_sum)
    p_low = p.astype(jnp.bfloat16)
    o = jnp.dot(p_low, v, preferred_element_type=jnp.float32)
    row_dot = jnp.sum(do.astype(jnp.float32) * o, axis=1, keepdims=True)
    dp = lax.dot_general(do, v, (((1,), (1,)), ((), ())),
                         preferred_element_type=jnp.float32)
    ds = (p * (dp - row_dot)).astype(jnp.bfloat16)
    dq = jnp.dot(ds, k, preferred_element_type=jnp.float32) * softmax_scale
    dk = lax.dot_general(ds, q, (((0,), (0,)), ((), ())),
                         preferred_element_type=jnp.float32) * softmax_scale
    dv = lax.dot_general(p_low, do, (((0,), (0,)), ((), ())),
                         preferred_element_type=jnp.float32)
    o_ref[:, :HEAD_SIZE] = o[:rows].astype(o_ref.dtype)
    o_ref[:, HEAD_SIZE:] = o[rows:].astype(o_ref.dtype)
    dq_ref[:, :HEAD_SIZE] = dq[:rows].astype(dq_ref.dtype)
    dq_ref[:, HEAD_SIZE:] = dq[rows:].astype(dq_ref.dtype)
    dk_ref[pl.ds(key_first, span), :] += dk
    dv_ref[pl.ds(key_first, span), :] += dv


def fused_attention(queries, extended, output_gradient, qdoc, kdoc, rows=BLK):
    tokens, query_cols = queries.shape
    ext_rows, joined_cols = extended.shape
    groups = joined_cols // (2 * HEAD_SIZE)
    blocks = tokens // rows
    span = rows + WIN
    pair = 2 * HEAD_SIZE
    flops = groups * blocks * 6 * 2 * (2 * rows) * span * HEAD_SIZE
    nbytes = 2 * (4 * tokens * query_cols + ext_rows * joined_cols) + 4 * ext_rows * joined_cols
    return pl.pallas_call(
        attention_kernel,
        grid=(groups, blocks),
        in_specs=[
            pl.BlockSpec((rows, pair), lambda g, b: (b, g)),
            pl.BlockSpec((ext_rows, HEAD_SIZE), lambda g, b: (0, g)),
            pl.BlockSpec((ext_rows, HEAD_SIZE), lambda g, b: (0, g + groups)),
            pl.BlockSpec((rows, pair), lambda g, b: (b, g)),
            pl.BlockSpec((rows, 1), lambda g, b: (b, 0)),
            pl.BlockSpec((1, ext_rows), lambda g, b: (0, 0)),
        ],
        out_specs=[
            pl.BlockSpec((rows, pair), lambda g, b: (b, g)),
            pl.BlockSpec((rows, pair), lambda g, b: (b, g)),
            pl.BlockSpec((ext_rows, HEAD_SIZE), lambda g, b: (0, g)),
            pl.BlockSpec((ext_rows, HEAD_SIZE), lambda g, b: (0, g)),
        ],
        out_shape=[
            jax.ShapeDtypeStruct((tokens, query_cols), jnp.bfloat16),
            jax.ShapeDtypeStruct((tokens, query_cols), jnp.bfloat16),
            jax.ShapeDtypeStruct((ext_rows, joined_cols // 2), jnp.float32),
            jax.ShapeDtypeStruct((ext_rows, joined_cols // 2), jnp.float32),
        ],
        compiler_params=pltpu.CompilerParams(
            dimension_semantics=("arbitrary", "arbitrary"),
            vmem_limit_bytes=48 * 1024 * 1024,
        ),
        cost_estimate=pl.CostEstimate(
            flops=flops, transcendentals=groups * blocks * 2 * rows * span,
            bytes_accessed=nbytes),
    )(queries, extended, extended, output_gradient, qdoc, kdoc)


def body(
    queries,
    key_head_tensor,
    value_head_tensor,
    output_gradient,
    adapter_up_matrix,
    document_block_counts,
):
    tokens_here = queries.shape[0]
    query_cols = queries.shape[1]
    key_cols = key_head_tensor.shape[1]
    edge_rows = min(WIN, tokens_here)
    hop_count = WIN // edge_rows
    first_pos = lax.axis_index("ctx") * tokens_here
    lowest = first_pos - WIN
    doc_ends = jnp.cumsum(document_block_counts) * BLK
    joined = jnp.concatenate([key_head_tensor, value_head_tensor], axis=1)
    arrived = []
    for hop_num in range(hop_count):
        arrived.append(passed_along(joined, "ctx", hop_num + 1))
    extended = jnp.concatenate(arrived[::-1] + [joined], axis=0)
    qdoc = doc_index(first_pos + jnp.arange(tokens_here, dtype=jnp.int32), doc_ends)
    kdoc = doc_index(lowest + jnp.arange(WIN + tokens_here, dtype=jnp.int32), doc_ends)
    attended, flattened_query, key_grads, value_grads = fused_attention(
        queries, extended, output_gradient, qdoc[:, None], kdoc[None, :]
    )
    halo_grads = jnp.concatenate([key_grads[:WIN], value_grads[:WIN]], axis=1)
    returned = jnp.zeros((edge_rows, 2 * key_cols), jnp.float32)
    for hop_num in range(hop_count):
        segment = halo_grads[
            (hop_count - 1 - hop_num) * edge_rows : (hop_count - hop_num) * edge_rows
        ]
        returned = returned + passed_along(
            segment.astype(jnp.bfloat16), "ctx", -(hop_num + 1)
        ).astype(segment.dtype)
    cut_row = tokens_here - edge_rows
    own = jnp.concatenate([key_grads[WIN:], value_grads[WIN:]], axis=1)
    total = jnp.concatenate([own[:cut_row], own[cut_row:] + returned], axis=0)
    key_total = total[:, :key_cols]
    value_total = total[:, key_cols:]
    adapter_portion = lax.dot_general(
        flattened_query,
        adapter_up_matrix,
        (((1,), (1,)), ((), ())),
        preferred_element_type=jnp.float32,
    )
    adapter_gradient = gathered_sum(adapter_portion, "head")
    return (
        attended,
        flattened_query,
        key_total.astype(jnp.bfloat16),
        value_total.astype(jnp.bfloat16),
        adapter_gradient,
    )


def solution(mesh):
    in_specs = (
        P("ctx", "head"),
        P("ctx", "head"),
        P("ctx", "head"),
        P("ctx", "head"),
        P(None, "head"),
        P(),
    )
    out_specs = (
        P("ctx", "head"),
        P("ctx", "head"),
        P("ctx", "head"),
        P("ctx", "head"),
        P("ctx", None),
    )
    return jax.shard_map(body, mesh=mesh, in_specs=in_specs, out_specs=out_specs, check_vma=False)
```

```python
import jax
import jax.numpy as jnp
from jax import lax
from jax.experimental import pallas as pl
from jax.experimental.pallas import tpu as pltpu
from jax.sharding import PartitionSpec as P

HEAD_SIZE = 128
WIN = 1024
BLK = 128


softmax_scale = 168.0 ** (-0.5)
masked_value = -1e30


def passed_along(block, axis, distance):
    devices = range(lax.axis_size(axis))
    route = [(i - distance, i) for i in devices if i - distance in devices]
    return lax.ppermute(block, axis, route)


def doc_index(positions, doc_ends):
    counted = jnp.sum((positions[:, None] >= doc_ends[None, :]).astype(jnp.int32), axis=1)
    return jnp.where(positions < 0, -1, counted)


def attention_kernel(q_ref, k_ref, v_ref, do_ref, qdoc_ref, kdoc_ref,
                     o_ref, dq_ref, dk_ref, dv_ref):
    qb = pl.program_id(1)
    rows = q_ref.shape[0]
    span = rows + WIN
    key_first = pl.multiple_of(qb * rows, rows)

    @pl.when(qb == 0)
    def _():
        dk_ref[...] = jnp.zeros_like(dk_ref)
        dv_ref[...] = jnp.zeros_like(dv_ref)

    q = jnp.concatenate([q_ref[:, :HEAD_SIZE], q_ref[:, HEAD_SIZE:]], axis=0)
    do = jnp.concatenate([do_ref[:, :HEAD_SIZE], do_ref[:, HEAD_SIZE:]], axis=0)
    k = k_ref[pl.ds(key_first, span), :]
    v = v_ref[pl.ds(key_first, span), :]
    qdoc = qdoc_ref[...]
    qdoc = jnp.concatenate([qdoc, qdoc], axis=0)
    kdoc = kdoc_ref[:, pl.ds(key_first, span)]
    row = lax.broadcasted_iota(jnp.int32, (2 * rows, span), 0) % rows
    col = lax.broadcasted_iota(jnp.int32, (2 * rows, span), 1)
    offset = row + WIN - col
    live = (offset >= 0) & (offset < WIN) & (qdoc == kdoc)

    s = lax.dot_general(q, k, (((1,), (1,)), ((), ())),
                        preferred_element_type=jnp.float32) * softmax_scale
    masked = jnp.where(live, s, masked_value)
    row_max = jnp.max(masked, axis=1, keepdims=True)
    e = jnp.exp(masked - row_max)
    row_sum = jnp.sum(e, axis=1, keepdims=True)
    p = e * (1.0 / row_sum)
    p_low = p.astype(jnp.bfloat16)
    o = jnp.dot(p_low, v, preferred_element_type=jnp.float32)
    row_dot = jnp.sum(do.astype(jnp.float32) * o, axis=1, keepdims=True)
    dp = lax.dot_general(do, v, (((1,), (1,)), ((), ())),
                         preferred_element_type=jnp.float32)
    ds = (p * (dp - row_dot)).astype(jnp.bfloat16)
    dq = jnp.dot(ds, k, preferred_element_type=jnp.float32) * softmax_scale
    dk = lax.dot_general(ds, q, (((0,), (0,)), ((), ())),
                         preferred_element_type=jnp.float32) * softmax_scale
    dv = lax.dot_general(p_low, do, (((0,), (0,)), ((), ())),
                         preferred_element_type=jnp.float32)
    o_ref[:, :HEAD_SIZE] = o[:rows].astype(o_ref.dtype)
    o_ref[:, HEAD_SIZE:] = o[rows:].astype(o_ref.dtype)
    dq_ref[:, :HEAD_SIZE] = dq[:rows].astype(dq_ref.dtype)
    dq_ref[:, HEAD_SIZE:] = dq[rows:].astype(dq_ref.dtype)
    dk_ref[pl.ds(key_first, span), :] += dk
    dv_ref[pl.ds(key_first, span), :] += dv


def fused_attention(queries, extended, output_gradient, qdoc, kdoc, rows=BLK):
    tokens, query_cols = queries.shape
    ext_rows, joined_cols = extended.shape
    groups = joined_cols // (2 * HEAD_SIZE)
    blocks = tokens // rows
    span = rows + WIN
    pair = 2 * HEAD_SIZE
    flops = groups * blocks * 6 * 2 * (2 * rows) * span * HEAD_SIZE
    nbytes = 2 * (4 * tokens * query_cols + ext_rows * joined_cols) + 4 * ext_rows * joined_cols
    return pl.pallas_call(
        attention_kernel,
        grid=(groups, blocks),
        in_specs=[
            pl.BlockSpec((rows, pair), lambda g, b: (b, g)),
            pl.BlockSpec((ext_rows, HEAD_SIZE), lambda g, b: (0, g)),
            pl.BlockSpec((ext_rows, HEAD_SIZE), lambda g, b: (0, g + groups)),
            pl.BlockSpec((rows, pair), lambda g, b: (b, g)),
            pl.BlockSpec((rows, 1), lambda g, b: (b, 0)),
            pl.BlockSpec((1, ext_rows), lambda g, b: (0, 0)),
        ],
        out_specs=[
            pl.BlockSpec((rows, pair), lambda g, b: (b, g)),
            pl.BlockSpec((rows, pair), lambda g, b: (b, g)),
            pl.BlockSpec((ext_rows, HEAD_SIZE), lambda g, b: (0, g)),
            pl.BlockSpec((ext_rows, HEAD_SIZE), lambda g, b: (0, g)),
        ],
        out_shape=[
            jax.ShapeDtypeStruct((tokens, query_cols), jnp.bfloat16),
            jax.ShapeDtypeStruct((tokens, query_cols), jnp.bfloat16),
            jax.ShapeDtypeStruct((ext_rows, joined_cols // 2), jnp.float32),
            jax.ShapeDtypeStruct((ext_rows, joined_cols // 2), jnp.float32),
        ],
        compiler_params=pltpu.CompilerParams(
            dimension_semantics=("arbitrary", "arbitrary"),
            vmem_limit_bytes=48 * 1024 * 1024,
        ),
        cost_estimate=pl.CostEstimate(
            flops=flops, transcendentals=groups * blocks * 2 * rows * span,
            bytes_accessed=nbytes),
    )(queries, extended, extended, output_gradient, qdoc, kdoc)


def body(
    queries,
    key_head_tensor,
    value_head_tensor,
    output_gradient,
    adapter_up_matrix,
    document_block_counts,
):
    tokens_here = queries.shape[0]
    query_cols = queries.shape[1]
    key_cols = key_head_tensor.shape[1]
    edge_rows = min(WIN, tokens_here)
    hop_count = WIN // edge_rows
    first_pos = lax.axis_index("ctx") * tokens_here
    lowest = first_pos - WIN
    doc_ends = jnp.cumsum(document_block_counts) * BLK
    joined = jnp.concatenate([key_head_tensor, value_head_tensor], axis=1)
    arrived = []
    for hop_num in range(hop_count):
        arrived.append(passed_along(joined, "ctx", hop_num + 1))
    extended = jnp.concatenate(arrived[::-1] + [joined], axis=0)
    qdoc = doc_index(first_pos + jnp.arange(tokens_here, dtype=jnp.int32), doc_ends)
    kdoc = doc_index(lowest + jnp.arange(WIN + tokens_here, dtype=jnp.int32), doc_ends)
    attended, flattened_query, key_grads, value_grads = fused_attention(
        queries, extended, output_gradient, qdoc[:, None], kdoc[None, :]
    )
    halo_grads = jnp.concatenate([key_grads[:WIN], value_grads[:WIN]], axis=1)
    returned = jnp.zeros((edge_rows, 2 * key_cols), jnp.float32)
    for hop_num in range(hop_count):
        segment = halo_grads[
            (hop_count - 1 - hop_num) * edge_rows : (hop_count - hop_num) * edge_rows
        ]
        returned = returned + passed_along(
            segment.astype(jnp.bfloat16), "ctx", -(hop_num + 1)
        ).astype(segment.dtype)
    cut_row = tokens_here - edge_rows
    own = jnp.concatenate([key_grads[WIN:], value_grads[WIN:]], axis=1)
    total = jnp.concatenate([own[:cut_row], own[cut_row:] + returned], axis=0)
    key_total = total[:, :key_cols]
    value_total = total[:, key_cols:]
    rank = adapter_up_matrix.shape[0]
    lane_rows = -(-rank // HEAD_SIZE) * HEAD_SIZE
    padded_up = jnp.pad(adapter_up_matrix, ((0, lane_rows - rank), (0, 0)))
    adapter_portion = lax.dot_general(
        flattened_query,
        padded_up,
        (((1,), (1,)), ((), ())),
        preferred_element_type=jnp.float32,
    )
    adapter_gradient = lax.psum(adapter_portion, "head")[:, :rank]
    return (
        attended,
        flattened_query,
        key_total.astype(jnp.bfloat16),
        value_total.astype(jnp.bfloat16),
        adapter_gradient,
    )


def solution(mesh):
    in_specs = (
        P("ctx", "head"),
        P("ctx", "head"),
        P("ctx", "head"),
        P("ctx", "head"),
        P(None, "head"),
        P(),
    )
    out_specs = (
        P("ctx", "head"),
        P("ctx", "head"),
        P("ctx", "head"),
        P("ctx", "head"),
        P("ctx", None),
    )
    return jax.shard_map(body, mesh=mesh, in_specs=in_specs, out_specs=out_specs, check_vma=False)
```

```python
import jax
import jax.numpy as jnp
from jax import lax
from jax.experimental import pallas as pl
from jax.experimental.pallas import tpu as pltpu
from jax.sharding import PartitionSpec as P

HEAD_SIZE = 128
WIN = 1024
BLK = 128


softmax_scale = 168.0 ** (-0.5)
masked_value = -1e30


def passed_along(block, axis, distance):
    devices = range(lax.axis_size(axis))
    route = [(i - distance, i) for i in devices if i - distance in devices]
    return lax.ppermute(block, axis, route)


def pairings(count):
    if count == 8:
        return [[i ^ 2 for i in range(8)], [(6 - i) % 8 if i % 2 == 0 else (8 - i) % 8 for i in range(8)], [i ^ 1 for i in range(8)]]
    rounds = []
    stride = 1
    while stride < count:
        rounds.append([i ^ stride for i in range(count)])
        stride *= 2
    return rounds


def gathered_sum(part, axis):
    total = part.astype(jnp.float32)
    for partner in pairings(lax.axis_size(axis)):
        route = [(i, partner[i]) for i in range(len(partner))]
        total = total + lax.ppermute(total, axis, route)
    return total


def doc_index(positions, doc_ends):
    counted = jnp.sum((positions[:, None] >= doc_ends[None, :]).astype(jnp.int32), axis=1)
    return jnp.where(positions < 0, -1, counted)


def attention_kernel(q_ref, k_ref, v_ref, do_ref, qdoc_ref, kdoc_ref,
                     o_ref, dq_ref, dk_ref, dv_ref):
    qb = pl.program_id(1)
    rows = q_ref.shape[0]
    span = rows + WIN
    key_first = pl.multiple_of(qb * rows, rows)

    @pl.when(qb == 0)
    def _():
        dk_ref[...] = jnp.zeros_like(dk_ref)
        dv_ref[...] = jnp.zeros_like(dv_ref)

    q = jnp.concatenate([q_ref[:, :HEAD_SIZE], q_ref[:, HEAD_SIZE:]], axis=0)
    do = jnp.concatenate([do_ref[:, :HEAD_SIZE], do_ref[:, HEAD_SIZE:]], axis=0)
    k = k_ref[pl.ds(key_first, span), :]
    v = v_ref[pl.ds(key_first, span), :]
    qdoc = qdoc_ref[...]
    qdoc = jnp.concatenate([qdoc, qdoc], axis=0)
    kdoc = kdoc_ref[:, pl.ds(key_first, span)]
    row = lax.broadcasted_iota(jnp.int32, (2 * rows, span), 0) % rows
    col = lax.broadcasted_iota(jnp.int32, (2 * rows, span), 1)
    offset = row + WIN - col
    live = (offset >= 0) & (offset < WIN) & (qdoc == kdoc)

    s = lax.dot_general(q, k, (((1,), (1,)), ((), ())),
                        preferred_element_type=jnp.float32) * softmax_scale
    masked = jnp.where(live, s, masked_value)
    row_max = jnp.max(masked, axis=1, keepdims=True)
    e = jnp.exp(masked - row_max)
    row_sum = jnp.sum(e, axis=1, keepdims=True)
    p = e * (1.0 / row_sum)
    p_low = p.astype(jnp.bfloat16)
    o = jnp.dot(p_low, v, preferred_element_type=jnp.float32)
    row_dot = jnp.sum(do.astype(jnp.float32) * o, axis=1, keepdims=True)
    dp = lax.dot_general(do, v, (((1,), (1,)), ((), ())),
                         preferred_element_type=jnp.float32)
    ds = (p * (dp - row_dot)).astype(jnp.bfloat16)
    dq = jnp.dot(ds, k, preferred_element_type=jnp.float32) * softmax_scale
    dk = lax.dot_general(ds, q, (((0,), (0,)), ((), ())),
                         preferred_element_type=jnp.float32) * softmax_scale
    dv = lax.dot_general(p_low, do, (((0,), (0,)), ((), ())),
                         preferred_element_type=jnp.float32)
    o_ref[:, :HEAD_SIZE] = o[:rows].astype(o_ref.dtype)
    o_ref[:, HEAD_SIZE:] = o[rows:].astype(o_ref.dtype)
    dq_ref[:, :HEAD_SIZE] = dq[:rows].astype(dq_ref.dtype)
    dq_ref[:, HEAD_SIZE:] = dq[rows:].astype(dq_ref.dtype)
    dk_ref[pl.ds(key_first, span), :] += dk
    dv_ref[pl.ds(key_first, span), :] += dv


def fused_attention(queries, extended, output_gradient, qdoc, kdoc, rows=BLK):
    tokens, query_cols = queries.shape
    ext_rows, joined_cols = extended.shape
    groups = joined_cols // (2 * HEAD_SIZE)
    blocks = tokens // rows
    span = rows + WIN
    pair = 2 * HEAD_SIZE
    flops = groups * blocks * 6 * 2 * (2 * rows) * span * HEAD_SIZE
    nbytes = 2 * (4 * tokens * query_cols + ext_rows * joined_cols) + 4 * ext_rows * joined_cols
    return pl.pallas_call(
        attention_kernel,
        grid=(groups, blocks),
        in_specs=[
            pl.BlockSpec((rows, pair), lambda g, b: (b, g)),
            pl.BlockSpec((ext_rows, HEAD_SIZE), lambda g, b: (0, g)),
            pl.BlockSpec((ext_rows, HEAD_SIZE), lambda g, b: (0, g + groups)),
            pl.BlockSpec((rows, pair), lambda g, b: (b, g)),
            pl.BlockSpec((rows, 1), lambda g, b: (b, 0)),
            pl.BlockSpec((1, ext_rows), lambda g, b: (0, 0)),
        ],
        out_specs=[
            pl.BlockSpec((rows, pair), lambda g, b: (b, g)),
            pl.BlockSpec((rows, pair), lambda g, b: (b, g)),
            pl.BlockSpec((ext_rows, HEAD_SIZE), lambda g, b: (0, g)),
            pl.BlockSpec((ext_rows, HEAD_SIZE), lambda g, b: (0, g)),
        ],
        out_shape=[
            jax.ShapeDtypeStruct((tokens, query_cols), jnp.bfloat16),
            jax.ShapeDtypeStruct((tokens, query_cols), jnp.bfloat16),
            jax.ShapeDtypeStruct((ext_rows, joined_cols // 2), jnp.float32),
            jax.ShapeDtypeStruct((ext_rows, joined_cols // 2), jnp.float32),
        ],
        compiler_params=pltpu.CompilerParams(
            dimension_semantics=("arbitrary", "arbitrary"),
            vmem_limit_bytes=48 * 1024 * 1024,
        ),
        cost_estimate=pl.CostEstimate(
            flops=flops, transcendentals=groups * blocks * 2 * rows * span,
            bytes_accessed=nbytes),
    )(queries, extended, extended, output_gradient, qdoc, kdoc)


def body(
    queries,
    key_head_tensor,
    value_head_tensor,
    output_gradient,
    adapter_up_matrix,
    document_block_counts,
):
    tokens_here = queries.shape[0]
    query_cols = queries.shape[1]
    key_cols = key_head_tensor.shape[1]
    edge_rows = min(WIN, tokens_here)
    hop_count = WIN // edge_rows
    first_pos = lax.axis_index("ctx") * tokens_here
    lowest = first_pos - WIN
    doc_ends = jnp.cumsum(document_block_counts) * BLK
    joined = jnp.concatenate([key_head_tensor, value_head_tensor], axis=1)
    arrived = []
    for hop_num in range(hop_count):
        arrived.append(passed_along(joined, "ctx", hop_num + 1))
    extended = jnp.concatenate(arrived[::-1] + [joined], axis=0)
    qdoc = doc_index(first_pos + jnp.arange(tokens_here, dtype=jnp.int32), doc_ends)
    kdoc = doc_index(lowest + jnp.arange(WIN + tokens_here, dtype=jnp.int32), doc_ends)
    attended, flattened_query, key_grads, value_grads = fused_attention(
        queries, extended, output_gradient, qdoc[:, None], kdoc[None, :]
    )
    halo_grads = jnp.concatenate([key_grads[:WIN], value_grads[:WIN]], axis=1)
    returned = jnp.zeros((edge_rows, 2 * key_cols), jnp.float32)
    for hop_num in range(hop_count):
        segment = halo_grads[
            (hop_count - 1 - hop_num) * edge_rows : (hop_count - hop_num) * edge_rows
        ]
        returned = returned + passed_along(
            segment.astype(jnp.bfloat16), "ctx", -(hop_num + 1)
        ).astype(segment.dtype)
    cut_row = tokens_here - edge_rows
    own = jnp.concatenate([key_grads[WIN:], value_grads[WIN:]], axis=1)
    total = jnp.concatenate([own[:cut_row], own[cut_row:] + returned], axis=0)
    key_total = total[:, :key_cols]
    value_total = total[:, key_cols:]
    adapter_portion = lax.dot_general(
        flattened_query,
        adapter_up_matrix,
        (((1,), (1,)), ((), ())),
        preferred_element_type=jnp.float32,
    )
    adapter_gradient = gathered_sum(adapter_portion, "head")
    return (
        attended,
        flattened_query,
        key_total.astype(jnp.bfloat16),
        value_total.astype(jnp.bfloat16),
        adapter_gradient,
    )


def solution(mesh):
    in_specs = (
        P("ctx", "head"),
        P("ctx", "head"),
        P("ctx", "head"),
        P("ctx", "head"),
        P(None, "head"),
        P(),
    )
    out_specs = (
        P("ctx", "head"),
        P("ctx", "head"),
        P("ctx", "head"),
        P("ctx", "head"),
        P("ctx", None),
    )
    return jax.shard_map(body, mesh=mesh, in_specs=in_specs, out_specs=out_specs, check_vma=False)
```

```python
import jax
import jax.numpy as jnp
from jax import lax
from jax.experimental import pallas as pl
from jax.experimental.pallas import tpu as pltpu
from jax.sharding import PartitionSpec as P

HEAD_SIZE = 128
WIN = 1024
BLK = 128


softmax_scale = 168.0 ** (-0.5)
masked_value = -1e30


def passed_along(block, axis, distance):
    devices = range(lax.axis_size(axis))
    route = [(i - distance, i) for i in devices if i - distance in devices]
    return lax.ppermute(block, axis, route)


def pairings(count):
    if count == 8:
        return [[i ^ 2 for i in range(8)], [(6 - i) % 8 if i % 2 == 0 else (8 - i) % 8 for i in range(8)], [i ^ 1 for i in range(8)]]
    rounds = []
    stride = 1
    while stride < count:
        rounds.append([i ^ stride for i in range(count)])
        stride *= 2
    return rounds


def gathered_sum(part, axis):
    total = part.astype(jnp.float32)
    for partner in pairings(lax.axis_size(axis)):
        route = [(i, partner[i]) for i in range(len(partner))]
        total = total + lax.ppermute(total, axis, route)
    return total


def doc_index(positions, doc_ends):
    counted = jnp.sum((positions[:, None] >= doc_ends[None, :]).astype(jnp.int32), axis=1)
    return jnp.where(positions < 0, -1, counted)


def attention_kernel(q_ref, k_ref, v_ref, do_ref, qdoc_ref, kdoc_ref, bias_ref,
                     o_ref, dq_ref, dk_ref, dv_ref):
    qb = pl.program_id(1)
    rows = q_ref.shape[0]
    span = rows + WIN
    key_first = pl.multiple_of(qb * rows, rows)

    @pl.when(qb == 0)
    def _():
        dk_ref[...] = jnp.zeros_like(dk_ref)
        dv_ref[...] = jnp.zeros_like(dv_ref)

    q = jnp.concatenate([q_ref[:, :HEAD_SIZE], q_ref[:, HEAD_SIZE:]], axis=0)
    do = jnp.concatenate([do_ref[:, :HEAD_SIZE], do_ref[:, HEAD_SIZE:]], axis=0)
    k = k_ref[pl.ds(key_first, span), :]
    v = v_ref[pl.ds(key_first, span), :]
    qdoc = qdoc_ref[...]
    qdoc = jnp.concatenate([qdoc, qdoc], axis=0)
    kdoc = kdoc_ref[:, pl.ds(key_first, span)]

    s = lax.dot_general(q, k, (((1,), (1,)), ((), ())),
                        preferred_element_type=jnp.float32) * softmax_scale
    masked = jnp.where(qdoc == kdoc, s + bias_ref[...], masked_value)
    row_max = jnp.max(masked, axis=1, keepdims=True)
    e = jnp.exp(masked - row_max)
    row_sum = jnp.sum(e, axis=1, keepdims=True)
    p = e * (1.0 / row_sum)
    p_low = p.astype(jnp.bfloat16)
    o = jnp.dot(p_low, v, preferred_element_type=jnp.float32)
    row_dot = jnp.sum(do.astype(jnp.float32) * o, axis=1, keepdims=True)
    dp = lax.dot_general(do, v, (((1,), (1,)), ((), ())),
                         preferred_element_type=jnp.float32)
    ds = (p * (dp - row_dot)).astype(jnp.bfloat16)
    dq = jnp.dot(ds, k, preferred_element_type=jnp.float32) * softmax_scale
    dk = lax.dot_general(ds, q, (((0,), (0,)), ((), ())),
                         preferred_element_type=jnp.float32) * softmax_scale
    dv = lax.dot_general(p_low, do, (((0,), (0,)), ((), ())),
                         preferred_element_type=jnp.float32)
    o_ref[:, :HEAD_SIZE] = o[:rows].astype(o_ref.dtype)
    o_ref[:, HEAD_SIZE:] = o[rows:].astype(o_ref.dtype)
    dq_ref[:, :HEAD_SIZE] = dq[:rows].astype(dq_ref.dtype)
    dq_ref[:, HEAD_SIZE:] = dq[rows:].astype(dq_ref.dtype)
    dk_ref[pl.ds(key_first, span), :] += dk
    dv_ref[pl.ds(key_first, span), :] += dv


def fused_attention(queries, extended, output_gradient, qdoc, kdoc, rows=BLK):
    tokens, query_cols = queries.shape
    ext_rows, joined_cols = extended.shape
    groups = joined_cols // (2 * HEAD_SIZE)
    blocks = tokens // rows
    span = rows + WIN
    pair = 2 * HEAD_SIZE
    flops = groups * blocks * 6 * 2 * (2 * rows) * span * HEAD_SIZE
    nbytes = 2 * (4 * tokens * query_cols + ext_rows * joined_cols) + 4 * ext_rows * joined_cols
    return pl.pallas_call(
        attention_kernel,
        grid=(groups, blocks),
        in_specs=[
            pl.BlockSpec((rows, pair), lambda g, b: (b, g)),
            pl.BlockSpec((ext_rows, HEAD_SIZE), lambda g, b: (0, g)),
            pl.BlockSpec((ext_rows, HEAD_SIZE), lambda g, b: (0, g + groups)),
            pl.BlockSpec((rows, pair), lambda g, b: (b, g)),
            pl.BlockSpec((rows, 1), lambda g, b: (b, 0)),
            pl.BlockSpec((1, ext_rows), lambda g, b: (0, 0)),
            pl.BlockSpec((2 * rows, span), lambda g, b: (0, 0)),
        ],
        out_specs=[
            pl.BlockSpec((rows, pair), lambda g, b: (b, g)),
            pl.BlockSpec((rows, pair), lambda g, b: (b, g)),
            pl.BlockSpec((ext_rows, HEAD_SIZE), lambda g, b: (0, g)),
            pl.BlockSpec((ext_rows, HEAD_SIZE), lambda g, b: (0, g)),
        ],
        out_shape=[
            jax.ShapeDtypeStruct((tokens, query_cols), jnp.bfloat16),
            jax.ShapeDtypeStruct((tokens, query_cols), jnp.bfloat16),
            jax.ShapeDtypeStruct((ext_rows, joined_cols // 2), jnp.float32),
            jax.ShapeDtypeStruct((ext_rows, joined_cols // 2), jnp.float32),
        ],
        compiler_params=pltpu.CompilerParams(
            dimension_semantics=("arbitrary", "arbitrary"),
            vmem_limit_bytes=48 * 1024 * 1024,
        ),
        cost_estimate=pl.CostEstimate(
            flops=flops, transcendentals=groups * blocks * 2 * rows * span,
            bytes_accessed=nbytes),
    )(queries, extended, extended, output_gradient, qdoc, kdoc, window_bias(rows))


def window_bias(rows):
    span = rows + WIN
    row = lax.broadcasted_iota(jnp.int32, (2 * rows, span), 0) % rows
    col = lax.broadcasted_iota(jnp.int32, (2 * rows, span), 1)
    offset = row + WIN - col
    inside = (offset >= 0) & (offset < WIN)
    return jnp.where(inside, 0.0, masked_value).astype(jnp.float32)


def body(
    queries,
    key_head_tensor,
    value_head_tensor,
    output_gradient,
    adapter_up_matrix,
    document_block_counts,
):
    tokens_here = queries.shape[0]
    query_cols = queries.shape[1]
    key_cols = key_head_tensor.shape[1]
    edge_rows = min(WIN, tokens_here)
    hop_count = WIN // edge_rows
    first_pos = lax.axis_index("ctx") * tokens_here
    lowest = first_pos - WIN
    doc_ends = jnp.cumsum(document_block_counts) * BLK
    joined = jnp.concatenate([key_head_tensor, value_head_tensor], axis=1)
    arrived = []
    for hop_num in range(hop_count):
        arrived.append(passed_along(joined, "ctx", hop_num + 1))
    extended = jnp.concatenate(arrived[::-1] + [joined], axis=0)
    qdoc = doc_index(first_pos + jnp.arange(tokens_here, dtype=jnp.int32), doc_ends)
    kdoc = doc_index(lowest + jnp.arange(WIN + tokens_here, dtype=jnp.int32), doc_ends)
    attended, flattened_query, key_grads, value_grads = fused_attention(
        queries, extended, output_gradient, qdoc[:, None], kdoc[None, :]
    )
    halo_grads = jnp.concatenate([key_grads[:WIN], value_grads[:WIN]], axis=1)
    returned = jnp.zeros((edge_rows, 2 * key_cols), jnp.float32)
    for hop_num in range(hop_count):
        segment = halo_grads[
            (hop_count - 1 - hop_num) * edge_rows : (hop_count - hop_num) * edge_rows
        ]
        returned = returned + passed_along(
            segment.astype(jnp.bfloat16), "ctx", -(hop_num + 1)
        ).astype(segment.dtype)
    cut_row = tokens_here - edge_rows
    own = jnp.concatenate([key_grads[WIN:], value_grads[WIN:]], axis=1)
    total = jnp.concatenate([own[:cut_row], own[cut_row:] + returned], axis=0)
    key_total = total[:, :key_cols]
    value_total = total[:, key_cols:]
    adapter_portion = lax.dot_general(
        flattened_query,
        adapter_up_matrix,
        (((1,), (1,)), ((), ())),
        preferred_element_type=jnp.float32,
    )
    adapter_gradient = gathered_sum(adapter_portion, "head")
    return (
        attended,
        flattened_query,
        key_total.astype(jnp.bfloat16),
        value_total.astype(jnp.bfloat16),
        adapter_gradient,
    )


def solution(mesh):
    in_specs = (
        P("ctx", "head"),
        P("ctx", "head"),
        P("ctx", "head"),
        P("ctx", "head"),
        P(None, "head"),
        P(),
    )
    out_specs = (
        P("ctx", "head"),
        P("ctx", "head"),
        P("ctx", "head"),
        P("ctx", "head"),
        P("ctx", None),
    )
    return jax.shard_map(body, mesh=mesh, in_specs=in_specs, out_specs=out_specs, check_vma=False)
```

```python
import jax
import jax.numpy as jnp
from jax import lax
from jax.experimental import pallas as pl
from jax.experimental.pallas import tpu as pltpu
from jax.sharding import PartitionSpec as P

HEAD_SIZE = 128
WIN = 1024
BLK = 128


softmax_scale = 168.0 ** (-0.5)
masked_value = -1e30


def passed_along(block, axis, distance):
    devices = range(lax.axis_size(axis))
    route = [(i - distance, i) for i in devices if i - distance in devices]
    return lax.ppermute(block, axis, route)


def pairings(count):
    if count == 8:
        return [[i ^ 2 for i in range(8)], [(6 - i) % 8 if i % 2 == 0 else (8 - i) % 8 for i in range(8)], [i ^ 1 for i in range(8)]]
    rounds = []
    stride = 1
    while stride < count:
        rounds.append([i ^ stride for i in range(count)])
        stride *= 2
    return rounds


def gathered_sum(part, axis):
    total = part.astype(jnp.float32)
    for partner in pairings(lax.axis_size(axis)):
        route = [(i, partner[i]) for i in range(len(partner))]
        total = total + lax.ppermute(total, axis, route)
    return total


def doc_index(positions, doc_ends):
    counted = jnp.sum((positions[:, None] >= doc_ends[None, :]).astype(jnp.int32), axis=1)
    return jnp.where(positions < 0, -1, counted)


def attention_kernel(q_ref, k_ref, v_ref, do_ref, qdoc_ref, kdoc_ref, bias_ref,
                     o_ref, dq_ref, dk_ref, dv_ref, dk_acc, dv_acc):
    qb = pl.program_id(1)
    rows = q_ref.shape[0]
    span = rows + WIN
    key_first = pl.multiple_of(qb * rows, rows)

    @pl.when(qb == 0)
    def _():
        dk_acc[...] = jnp.zeros_like(dk_acc)
        dv_acc[...] = jnp.zeros_like(dv_acc)

    q = jnp.concatenate([q_ref[:, :HEAD_SIZE], q_ref[:, HEAD_SIZE:]], axis=0)
    do = jnp.concatenate([do_ref[:, :HEAD_SIZE], do_ref[:, HEAD_SIZE:]], axis=0)
    k = k_ref[pl.ds(key_first, span), :]
    v = v_ref[pl.ds(key_first, span), :]
    qdoc = qdoc_ref[...]
    qdoc = jnp.concatenate([qdoc, qdoc], axis=0)
    kdoc = kdoc_ref[:, pl.ds(key_first, span)]

    s = lax.dot_general(q, k, (((1,), (1,)), ((), ())),
                        preferred_element_type=jnp.float32) * softmax_scale
    masked = jnp.where(qdoc == kdoc, s + bias_ref[...], masked_value)
    row_max = jnp.max(masked, axis=1, keepdims=True)
    e = jnp.exp(masked - row_max)
    row_sum = jnp.sum(e, axis=1, keepdims=True)
    p = e * (1.0 / row_sum)
    p_low = p.astype(jnp.bfloat16)
    o = jnp.dot(p_low, v, preferred_element_type=jnp.float32)
    row_dot = jnp.sum(do.astype(jnp.float32) * o, axis=1, keepdims=True)
    dp = lax.dot_general(do, v, (((1,), (1,)), ((), ())),
                         preferred_element_type=jnp.float32)
    ds = (p * (dp - row_dot)).astype(jnp.bfloat16)
    dq = jnp.dot(ds, k, preferred_element_type=jnp.float32) * softmax_scale
    dk = jnp.dot(q.T, ds, preferred_element_type=jnp.float32) * softmax_scale
    dv = jnp.dot(do.T, p_low, preferred_element_type=jnp.float32)
    o_ref[:, :HEAD_SIZE] = o[:rows].astype(o_ref.dtype)
    o_ref[:, HEAD_SIZE:] = o[rows:].astype(o_ref.dtype)
    dq_ref[:, :HEAD_SIZE] = dq[:rows].astype(dq_ref.dtype)
    dq_ref[:, HEAD_SIZE:] = dq[rows:].astype(dq_ref.dtype)
    dk_acc[:, pl.ds(key_first, span)] += dk
    dv_acc[:, pl.ds(key_first, span)] += dv

    @pl.when(qb == pl.num_programs(1) - 1)
    def _():
        dk_ref[...] = dk_acc[...].T
        dv_ref[...] = dv_acc[...].T


def fused_attention(queries, extended, output_gradient, qdoc, kdoc, rows=BLK):
    tokens, query_cols = queries.shape
    ext_rows, joined_cols = extended.shape
    groups = joined_cols // (2 * HEAD_SIZE)
    blocks = tokens // rows
    span = rows + WIN
    pair = 2 * HEAD_SIZE
    flops = groups * blocks * 6 * 2 * (2 * rows) * span * HEAD_SIZE
    nbytes = 2 * (4 * tokens * query_cols + ext_rows * joined_cols) + 4 * ext_rows * joined_cols
    return pl.pallas_call(
        attention_kernel,
        grid=(groups, blocks),
        in_specs=[
            pl.BlockSpec((rows, pair), lambda g, b: (b, g)),
            pl.BlockSpec((ext_rows, HEAD_SIZE), lambda g, b: (0, g)),
            pl.BlockSpec((ext_rows, HEAD_SIZE), lambda g, b: (0, g + groups)),
            pl.BlockSpec((rows, pair), lambda g, b: (b, g)),
            pl.BlockSpec((rows, 1), lambda g, b: (b, 0)),
            pl.BlockSpec((1, ext_rows), lambda g, b: (0, 0)),
            pl.BlockSpec((2 * rows, span), lambda g, b: (0, 0)),
        ],
        out_specs=[
            pl.BlockSpec((rows, pair), lambda g, b: (b, g)),
            pl.BlockSpec((rows, pair), lambda g, b: (b, g)),
            pl.BlockSpec((ext_rows, HEAD_SIZE), lambda g, b: (0, g)),
            pl.BlockSpec((ext_rows, HEAD_SIZE), lambda g, b: (0, g)),
        ],
        out_shape=[
            jax.ShapeDtypeStruct((tokens, query_cols), jnp.bfloat16),
            jax.ShapeDtypeStruct((tokens, query_cols), jnp.bfloat16),
            jax.ShapeDtypeStruct((ext_rows, joined_cols // 2), jnp.float32),
            jax.ShapeDtypeStruct((ext_rows, joined_cols // 2), jnp.float32),
        ],
        scratch_shapes=[
            pltpu.VMEM((HEAD_SIZE, ext_rows), jnp.float32),
            pltpu.VMEM((HEAD_SIZE, ext_rows), jnp.float32),
        ],
        compiler_params=pltpu.CompilerParams(
            dimension_semantics=("arbitrary", "arbitrary"),
            vmem_limit_bytes=48 * 1024 * 1024,
        ),
        cost_estimate=pl.CostEstimate(
            flops=flops, transcendentals=groups * blocks * 2 * rows * span,
            bytes_accessed=nbytes),
    )(queries, extended, extended, output_gradient, qdoc, kdoc, window_bias(rows))


def window_bias(rows):
    span = rows + WIN
    row = lax.broadcasted_iota(jnp.int32, (2 * rows, span), 0) % rows
    col = lax.broadcasted_iota(jnp.int32, (2 * rows, span), 1)
    offset = row + WIN - col
    inside = (offset >= 0) & (offset < WIN)
    return jnp.where(inside, 0.0, masked_value).astype(jnp.float32)


def body(
    queries,
    key_head_tensor,
    value_head_tensor,
    output_gradient,
    adapter_up_matrix,
    document_block_counts,
):
    tokens_here = queries.shape[0]
    query_cols = queries.shape[1]
    key_cols = key_head_tensor.shape[1]
    edge_rows = min(WIN, tokens_here)
    hop_count = WIN // edge_rows
    first_pos = lax.axis_index("ctx") * tokens_here
    lowest = first_pos - WIN
    doc_ends = jnp.cumsum(document_block_counts) * BLK
    joined = jnp.concatenate([key_head_tensor, value_head_tensor], axis=1)
    arrived = []
    for hop_num in range(hop_count):
        arrived.append(passed_along(joined, "ctx", hop_num + 1))
    extended = jnp.concatenate(arrived[::-1] + [joined], axis=0)
    qdoc = doc_index(first_pos + jnp.arange(tokens_here, dtype=jnp.int32), doc_ends)
    kdoc = doc_index(lowest + jnp.arange(WIN + tokens_here, dtype=jnp.int32), doc_ends)
    attended, flattened_query, key_grads, value_grads = fused_attention(
        queries, extended, output_gradient, qdoc[:, None], kdoc[None, :]
    )
    halo_grads = jnp.concatenate([key_grads[:WIN], value_grads[:WIN]], axis=1)
    returned = jnp.zeros((edge_rows, 2 * key_cols), jnp.float32)
    for hop_num in range(hop_count):
        segment = halo_grads[
            (hop_count - 1 - hop_num) * edge_rows : (hop_count - hop_num) * edge_rows
        ]
        returned = returned + passed_along(
            segment.astype(jnp.bfloat16), "ctx", -(hop_num + 1)
        ).astype(segment.dtype)
    cut_row = tokens_here - edge_rows
    own = jnp.concatenate([key_grads[WIN:], value_grads[WIN:]], axis=1)
    total = jnp.concatenate([own[:cut_row], own[cut_row:] + returned], axis=0)
    key_total = total[:, :key_cols]
    value_total = total[:, key_cols:]
    adapter_portion = lax.dot_general(
        flattened_query,
        adapter_up_matrix,
        (((1,), (1,)), ((), ())),
        preferred_element_type=jnp.float32,
    )
    adapter_gradient = gathered_sum(adapter_portion, "head")
    return (
        attended,
        flattened_query,
        key_total.astype(jnp.bfloat16),
        value_total.astype(jnp.bfloat16),
        adapter_gradient,
    )


def solution(mesh):
    in_specs = (
        P("ctx", "head"),
        P("ctx", "head"),
        P("ctx", "head"),
        P("ctx", "head"),
        P(None, "head"),
        P(),
    )
    out_specs = (
        P("ctx", "head"),
        P("ctx", "head"),
        P("ctx", "head"),
        P("ctx", "head"),
        P("ctx", None),
    )
    return jax.shard_map(body, mesh=mesh, in_specs=in_specs, out_specs=out_specs, check_vma=False)
```

```python
import jax
import jax.numpy as jnp
from jax import lax
from jax.experimental import pallas as pl
from jax.experimental.pallas import tpu as pltpu
from jax.sharding import PartitionSpec as P

HEAD_SIZE = 128
WIN = 1024
BLK = 128


softmax_scale = 168.0 ** (-0.5)
masked_value = -1e30


def passed_along(block, axis, distance):
    devices = range(lax.axis_size(axis))
    route = [(i - distance, i) for i in devices if i - distance in devices]
    return lax.ppermute(block, axis, route)


def pairings(count):
    if count == 8:
        return [[i ^ 2 for i in range(8)], [(6 - i) % 8 if i % 2 == 0 else (8 - i) % 8 for i in range(8)], [i ^ 1 for i in range(8)]]
    rounds = []
    stride = 1
    while stride < count:
        rounds.append([i ^ stride for i in range(count)])
        stride *= 2
    return rounds


def gathered_sum(part, axis):
    total = part.astype(jnp.float32)
    for partner in pairings(lax.axis_size(axis)):
        route = [(i, partner[i]) for i in range(len(partner))]
        total = total + lax.ppermute(total, axis, route)
    return total


def doc_index(positions, doc_ends):
    counted = jnp.sum((positions[:, None] >= doc_ends[None, :]).astype(jnp.int32), axis=1)
    return jnp.where(positions < 0, -1, counted)


def attention_kernel(q_ref, k_ref, v_ref, do_ref, qdoc_ref, kdoc_ref, bias_ref,
                     o_ref, dq_ref, dk_ref, dv_ref, dk_acc, dv_acc):
    qb = pl.program_id(1)
    rows = q_ref.shape[0]
    span = rows + WIN
    key_first = pl.multiple_of(qb * rows, rows)

    @pl.when(qb == 0)
    def _():
        dk_acc[...] = jnp.zeros_like(dk_acc)
        dv_acc[...] = jnp.zeros_like(dv_acc)

    q = jnp.concatenate([q_ref[:, :HEAD_SIZE], q_ref[:, HEAD_SIZE:]], axis=0)
    do = jnp.concatenate([do_ref[:, :HEAD_SIZE], do_ref[:, HEAD_SIZE:]], axis=0)
    k = k_ref[pl.ds(key_first, span), :]
    v = v_ref[pl.ds(key_first, span), :]
    qdoc = qdoc_ref[...]
    qdoc = jnp.concatenate([qdoc, qdoc], axis=0)
    kdoc = kdoc_ref[:, pl.ds(key_first, span)]

    s = lax.dot_general(q, k, (((1,), (1,)), ((), ())),
                        preferred_element_type=jnp.float32) * softmax_scale
    masked = jnp.where(qdoc == kdoc, s + bias_ref[...], masked_value)
    row_max = jnp.max(masked, axis=1, keepdims=True)
    e = jnp.exp(masked - row_max)
    row_sum = jnp.sum(e, axis=1, keepdims=True)
    p = e * (1.0 / row_sum)
    p_low = p.astype(jnp.bfloat16)
    o = jnp.dot(p_low, v, preferred_element_type=jnp.float32)
    row_dot = jnp.sum(do.astype(jnp.float32) * o, axis=1, keepdims=True)
    dp = lax.dot_general(do, v, (((1,), (1,)), ((), ())),
                         preferred_element_type=jnp.float32)
    ds = (p * (dp - row_dot)).astype(jnp.bfloat16)
    dq = jnp.dot(ds, k, preferred_element_type=jnp.float32) * softmax_scale
    dk = jnp.dot(q.T, ds, preferred_element_type=jnp.float32) * softmax_scale
    dv = jnp.dot(do.T, p_low, preferred_element_type=jnp.float32)
    o_ref[:, :HEAD_SIZE] = o[:rows].astype(o_ref.dtype)
    o_ref[:, HEAD_SIZE:] = o[rows:].astype(o_ref.dtype)
    dq_ref[:, :HEAD_SIZE] = dq[:rows].astype(dq_ref.dtype)
    dq_ref[:, HEAD_SIZE:] = dq[rows:].astype(dq_ref.dtype)
    dk_acc[:, pl.ds(key_first, span)] += dk
    dv_acc[:, pl.ds(key_first, span)] += dv

    @pl.when(qb == pl.num_programs(1) - 1)
    def _():
        dk_ref[...] = dk_acc[...].T
        dv_ref[...] = dv_acc[...].T


def fused_attention(queries, extended, output_gradient, qdoc, kdoc, rows=2 * BLK):
    tokens, query_cols = queries.shape
    ext_rows, joined_cols = extended.shape
    groups = joined_cols // (2 * HEAD_SIZE)
    blocks = tokens // rows
    span = rows + WIN
    pair = 2 * HEAD_SIZE
    flops = groups * blocks * 6 * 2 * (2 * rows) * span * HEAD_SIZE
    nbytes = 2 * (4 * tokens * query_cols + ext_rows * joined_cols) + 4 * ext_rows * joined_cols
    return pl.pallas_call(
        attention_kernel,
        grid=(groups, blocks),
        in_specs=[
            pl.BlockSpec((rows, pair), lambda g, b: (b, g)),
            pl.BlockSpec((ext_rows, HEAD_SIZE), lambda g, b: (0, g)),
            pl.BlockSpec((ext_rows, HEAD_SIZE), lambda g, b: (0, g + groups)),
            pl.BlockSpec((rows, pair), lambda g, b: (b, g)),
            pl.BlockSpec((rows, 1), lambda g, b: (b, 0)),
            pl.BlockSpec((1, ext_rows), lambda g, b: (0, 0)),
            pl.BlockSpec((2 * rows, span), lambda g, b: (0, 0)),
        ],
        out_specs=[
            pl.BlockSpec((rows, pair), lambda g, b: (b, g)),
            pl.BlockSpec((rows, pair), lambda g, b: (b, g)),
            pl.BlockSpec((ext_rows, HEAD_SIZE), lambda g, b: (0, g)),
            pl.BlockSpec((ext_rows, HEAD_SIZE), lambda g, b: (0, g)),
        ],
        out_shape=[
            jax.ShapeDtypeStruct((tokens, query_cols), jnp.bfloat16),
            jax.ShapeDtypeStruct((tokens, query_cols), jnp.bfloat16),
            jax.ShapeDtypeStruct((ext_rows, joined_cols // 2), jnp.float32),
            jax.ShapeDtypeStruct((ext_rows, joined_cols // 2), jnp.float32),
        ],
        scratch_shapes=[
            pltpu.VMEM((HEAD_SIZE, ext_rows), jnp.float32),
            pltpu.VMEM((HEAD_SIZE, ext_rows), jnp.float32),
        ],
        compiler_params=pltpu.CompilerParams(
            dimension_semantics=("arbitrary", "arbitrary"),
            vmem_limit_bytes=48 * 1024 * 1024,
        ),
        cost_estimate=pl.CostEstimate(
            flops=flops, transcendentals=groups * blocks * 2 * rows * span,
            bytes_accessed=nbytes),
    )(queries, extended, extended, output_gradient, qdoc, kdoc, window_bias(rows))


def window_bias(rows):
    span = rows + WIN
    row = lax.broadcasted_iota(jnp.int32, (2 * rows, span), 0) % rows
    col = lax.broadcasted_iota(jnp.int32, (2 * rows, span), 1)
    offset = row + WIN - col
    inside = (offset >= 0) & (offset < WIN)
    return jnp.where(inside, 0.0, masked_value).astype(jnp.float32)


def body(
    queries,
    key_head_tensor,
    value_head_tensor,
    output_gradient,
    adapter_up_matrix,
    document_block_counts,
):
    tokens_here = queries.shape[0]
    query_cols = queries.shape[1]
    key_cols = key_head_tensor.shape[1]
    edge_rows = min(WIN, tokens_here)
    hop_count = WIN // edge_rows
    first_pos = lax.axis_index("ctx") * tokens_here
    lowest = first_pos - WIN
    doc_ends = jnp.cumsum(document_block_counts) * BLK
    joined = jnp.concatenate([key_head_tensor, value_head_tensor], axis=1)
    arrived = []
    for hop_num in range(hop_count):
        arrived.append(passed_along(joined, "ctx", hop_num + 1))
    extended = jnp.concatenate(arrived[::-1] + [joined], axis=0)
    qdoc = doc_index(first_pos + jnp.arange(tokens_here, dtype=jnp.int32), doc_ends)
    kdoc = doc_index(lowest + jnp.arange(WIN + tokens_here, dtype=jnp.int32), doc_ends)
    attended, flattened_query, key_grads, value_grads = fused_attention(
        queries, extended, output_gradient, qdoc[:, None], kdoc[None, :]
    )
    halo_grads = jnp.concatenate([key_grads[:WIN], value_grads[:WIN]], axis=1)
    returned = jnp.zeros((edge_rows, 2 * key_cols), jnp.float32)
    for hop_num in range(hop_count):
        segment = halo_grads[
            (hop_count - 1 - hop_num) * edge_rows : (hop_count - hop_num) * edge_rows
        ]
        returned = returned + passed_along(
            segment.astype(jnp.bfloat16), "ctx", -(hop_num + 1)
        ).astype(segment.dtype)
    cut_row = tokens_here - edge_rows
    own = jnp.concatenate([key_grads[WIN:], value_grads[WIN:]], axis=1)
    total = jnp.concatenate([own[:cut_row], own[cut_row:] + returned], axis=0)
    key_total = total[:, :key_cols]
    value_total = total[:, key_cols:]
    adapter_portion = lax.dot_general(
        flattened_query,
        adapter_up_matrix,
        (((1,), (1,)), ((), ())),
        preferred_element_type=jnp.float32,
    )
    adapter_gradient = gathered_sum(adapter_portion, "head")
    return (
        attended,
        flattened_query,
        key_total.astype(jnp.bfloat16),
        value_total.astype(jnp.bfloat16),
        adapter_gradient,
    )


def solution(mesh):
    in_specs = (
        P("ctx", "head"),
        P("ctx", "head"),
        P("ctx", "head"),
        P("ctx", "head"),
        P(None, "head"),
        P(),
    )
    out_specs = (
        P("ctx", "head"),
        P("ctx", "head"),
        P("ctx", "head"),
        P("ctx", "head"),
        P("ctx", None),
    )
    return jax.shard_map(body, mesh=mesh, in_specs=in_specs, out_specs=out_specs, check_vma=False)
```

```python
import jax
import jax.numpy as jnp
from jax import lax
from jax.experimental import pallas as pl
from jax.experimental.pallas import tpu as pltpu
from jax.sharding import PartitionSpec as P

HEAD_SIZE = 128
WIN = 1024
BLK = 128


softmax_scale = 168.0 ** (-0.5)
masked_value = -1e30


def passed_along(block, axis, distance):
    devices = range(lax.axis_size(axis))
    route = [(i - distance, i) for i in devices if i - distance in devices]
    return lax.ppermute(block, axis, route)


def pairings(count):
    if count == 8:
        return [[i ^ 2 for i in range(8)], [(6 - i) % 8 if i % 2 == 0 else (8 - i) % 8 for i in range(8)], [i ^ 1 for i in range(8)]]
    rounds = []
    stride = 1
    while stride < count:
        rounds.append([i ^ stride for i in range(count)])
        stride *= 2
    return rounds


def gathered_sum(part, axis):
    total = part.astype(jnp.float32)
    for partner in pairings(lax.axis_size(axis)):
        route = [(i, partner[i]) for i in range(len(partner))]
        total = total + lax.ppermute(total, axis, route)
    return total


def doc_index(positions, doc_ends):
    counted = jnp.sum((positions[:, None] >= doc_ends[None, :]).astype(jnp.int32), axis=1)
    return jnp.where(positions < 0, -1, counted)


def attention_kernel(q_ref, k_ref, v_ref, do_ref, qdoc_ref, kdoc_ref, bias_ref,
                     o_ref, dq_ref, dk_ref, dv_ref, dk_acc, dv_acc):
    qb = pl.program_id(1)
    rows = q_ref.shape[0]
    span = rows + WIN
    key_first = pl.multiple_of(qb * rows, rows)

    @pl.when(qb == 0)
    def _():
        dk_acc[...] = jnp.zeros_like(dk_acc)
        dv_acc[...] = jnp.zeros_like(dv_acc)

    q = jnp.concatenate([q_ref[:, :HEAD_SIZE], q_ref[:, HEAD_SIZE:]], axis=0)
    do = jnp.concatenate([do_ref[:, :HEAD_SIZE], do_ref[:, HEAD_SIZE:]], axis=0)
    k = k_ref[pl.ds(key_first, span), :]
    v = v_ref[pl.ds(key_first, span), :]
    qdoc = qdoc_ref[...]
    qdoc = jnp.concatenate([qdoc, qdoc], axis=0)
    kdoc = kdoc_ref[:, pl.ds(key_first, span)]

    s = lax.dot_general(q, k, (((1,), (1,)), ((), ())),
                        preferred_element_type=jnp.float32) * softmax_scale
    masked = jnp.where(qdoc == kdoc, s + bias_ref[...], masked_value)
    row_max = jnp.max(masked, axis=1, keepdims=True)
    e = jnp.exp(masked - row_max)
    row_sum = jnp.sum(e, axis=1, keepdims=True)
    p = e * (1.0 / row_sum)
    p_low = p.astype(jnp.bfloat16)
    o = jnp.dot(p_low, v, preferred_element_type=jnp.float32)
    row_dot = jnp.sum(do.astype(jnp.float32) * o, axis=1, keepdims=True)
    dp = lax.dot_general(do, v, (((1,), (1,)), ((), ())),
                         preferred_element_type=jnp.float32)
    ds = (p * (dp - row_dot)).astype(jnp.bfloat16)
    dq = jnp.dot(ds, k, preferred_element_type=jnp.float32) * softmax_scale
    dk = jnp.dot(q.T, ds, preferred_element_type=jnp.float32) * softmax_scale
    dv = jnp.dot(do.T, p_low, preferred_element_type=jnp.float32)
    o_ref[:, :HEAD_SIZE] = o[:rows].astype(o_ref.dtype)
    o_ref[:, HEAD_SIZE:] = o[rows:].astype(o_ref.dtype)
    dq_ref[:, :HEAD_SIZE] = dq[:rows].astype(dq_ref.dtype)
    dq_ref[:, HEAD_SIZE:] = dq[rows:].astype(dq_ref.dtype)
    dk_acc[:, pl.ds(key_first, span)] += dk
    dv_acc[:, pl.ds(key_first, span)] += dv

    @pl.when(qb == pl.num_programs(1) - 1)
    def _():
        dk_ref[...] = dk_acc[...].T
        dv_ref[...] = dv_acc[...].T


def fused_attention(queries, extended, output_gradient, qdoc, kdoc, rows=2 * BLK):
    tokens, query_cols = queries.shape
    ext_rows, joined_cols = extended.shape
    groups = joined_cols // (2 * HEAD_SIZE)
    blocks = tokens // rows
    span = rows + WIN
    pair = 2 * HEAD_SIZE
    flops = groups * blocks * 6 * 2 * (2 * rows) * span * HEAD_SIZE
    nbytes = 2 * (4 * tokens * query_cols + ext_rows * joined_cols) + 4 * ext_rows * joined_cols
    return pl.pallas_call(
        attention_kernel,
        grid=(groups, blocks),
        in_specs=[
            pl.BlockSpec((rows, pair), lambda g, b: (b, g)),
            pl.BlockSpec((ext_rows, HEAD_SIZE), lambda g, b: (0, g)),
            pl.BlockSpec((ext_rows, HEAD_SIZE), lambda g, b: (0, g + groups)),
            pl.BlockSpec((rows, pair), lambda g, b: (b, g)),
            pl.BlockSpec((rows, 1), lambda g, b: (b, 0)),
            pl.BlockSpec((1, ext_rows), lambda g, b: (0, 0)),
            pl.BlockSpec((2 * rows, span), lambda g, b: (0, 0)),
        ],
        out_specs=[
            pl.BlockSpec((rows, pair), lambda g, b: (b, g)),
            pl.BlockSpec((rows, pair), lambda g, b: (b, g)),
            pl.BlockSpec((ext_rows, HEAD_SIZE), lambda g, b: (0, g)),
            pl.BlockSpec((ext_rows, HEAD_SIZE), lambda g, b: (0, g)),
        ],
        out_shape=[
            jax.ShapeDtypeStruct((tokens, query_cols), jnp.bfloat16),
            jax.ShapeDtypeStruct((tokens, query_cols), jnp.bfloat16),
            jax.ShapeDtypeStruct((ext_rows, joined_cols // 2), jnp.float32),
            jax.ShapeDtypeStruct((ext_rows, joined_cols // 2), jnp.float32),
        ],
        scratch_shapes=[
            pltpu.VMEM((HEAD_SIZE, ext_rows), jnp.float32),
            pltpu.VMEM((HEAD_SIZE, ext_rows), jnp.float32),
        ],
        compiler_params=pltpu.CompilerParams(
            dimension_semantics=("arbitrary", "arbitrary"),
            vmem_limit_bytes=48 * 1024 * 1024,
        ),
        cost_estimate=pl.CostEstimate(
            flops=flops, transcendentals=groups * blocks * 2 * rows * span,
            bytes_accessed=nbytes),
    )(queries, extended, extended, output_gradient, qdoc, kdoc, window_bias(rows))


def window_bias(rows):
    span = rows + WIN
    row = lax.broadcasted_iota(jnp.int32, (2 * rows, span), 0) % rows
    col = lax.broadcasted_iota(jnp.int32, (2 * rows, span), 1)
    offset = row + WIN - col
    inside = (offset >= 0) & (offset < WIN)
    return jnp.where(inside, 0.0, masked_value).astype(jnp.float32)


def join_kernel(k_ref, v_ref, o_ref):
    cols = k_ref.shape[1]
    o_ref[:, :cols] = k_ref[...]
    o_ref[:, cols:] = v_ref[...]


def joined_columns(keys, values):
    rows, cols = keys.shape
    return pl.pallas_call(
        join_kernel,
        out_shape=jax.ShapeDtypeStruct((rows, 2 * cols), keys.dtype),
        cost_estimate=pl.CostEstimate(
            flops=0, transcendentals=0, bytes_accessed=4 * rows * cols * keys.dtype.itemsize),
    )(keys, values)


def body(
    queries,
    key_head_tensor,
    value_head_tensor,
    output_gradient,
    adapter_up_matrix,
    document_block_counts,
):
    tokens_here = queries.shape[0]
    query_cols = queries.shape[1]
    key_cols = key_head_tensor.shape[1]
    edge_rows = min(WIN, tokens_here)
    hop_count = WIN // edge_rows
    first_pos = lax.axis_index("ctx") * tokens_here
    lowest = first_pos - WIN
    doc_ends = jnp.cumsum(document_block_counts) * BLK
    joined = joined_columns(key_head_tensor, value_head_tensor)
    arrived = []
    for hop_num in range(hop_count):
        arrived.append(passed_along(joined, "ctx", hop_num + 1))
    extended = jnp.concatenate(arrived[::-1] + [joined], axis=0)
    qdoc = doc_index(first_pos + jnp.arange(tokens_here, dtype=jnp.int32), doc_ends)
    kdoc = doc_index(lowest + jnp.arange(WIN + tokens_here, dtype=jnp.int32), doc_ends)
    attended, flattened_query, key_grads, value_grads = fused_attention(
        queries, extended, output_gradient, qdoc[:, None], kdoc[None, :]
    )
    halo_grads = jnp.concatenate([key_grads[:WIN], value_grads[:WIN]], axis=1)
    returned = jnp.zeros((edge_rows, 2 * key_cols), jnp.float32)
    for hop_num in range(hop_count):
        segment = halo_grads[
            (hop_count - 1 - hop_num) * edge_rows : (hop_count - hop_num) * edge_rows
        ]
        returned = returned + passed_along(
            segment.astype(jnp.bfloat16), "ctx", -(hop_num + 1)
        ).astype(segment.dtype)
    cut_row = tokens_here - edge_rows
    own = jnp.concatenate([key_grads[WIN:], value_grads[WIN:]], axis=1)
    total = jnp.concatenate([own[:cut_row], own[cut_row:] + returned], axis=0)
    key_total = total[:, :key_cols]
    value_total = total[:, key_cols:]
    adapter_portion = lax.dot_general(
        flattened_query,
        adapter_up_matrix,
        (((1,), (1,)), ((), ())),
        preferred_element_type=jnp.float32,
    )
    adapter_gradient = gathered_sum(adapter_portion, "head")
    return (
        attended,
        flattened_query,
        key_total.astype(jnp.bfloat16),
        value_total.astype(jnp.bfloat16),
        adapter_gradient,
    )


def solution(mesh):
    in_specs = (
        P("ctx", "head"),
        P("ctx", "head"),
        P("ctx", "head"),
        P("ctx", "head"),
        P(None, "head"),
        P(),
    )
    out_specs = (
        P("ctx", "head"),
        P("ctx", "head"),
        P("ctx", "head"),
        P("ctx", "head"),
        P("ctx", None),
    )
    return jax.shard_map(body, mesh=mesh, in_specs=in_specs, out_specs=out_specs, check_vma=False)
```

```python
import jax
import jax.numpy as jnp
from jax import lax
from jax.experimental import pallas as pl
from jax.experimental.pallas import tpu as pltpu
from jax.sharding import PartitionSpec as P

HEAD_SIZE = 128
WIN = 1024
BLK = 128


softmax_scale = 168.0 ** (-0.5)
masked_value = -1e30


def passed_along(block, axis, distance):
    devices = range(lax.axis_size(axis))
    route = [(i - distance, i) for i in devices if i - distance in devices]
    return lax.ppermute(block, axis, route)


def pairings(count):
    if count == 8:
        return [[i ^ 2 for i in range(8)], [(6 - i) % 8 if i % 2 == 0 else (8 - i) % 8 for i in range(8)], [i ^ 1 for i in range(8)]]
    rounds = []
    stride = 1
    while stride < count:
        rounds.append([i ^ stride for i in range(count)])
        stride *= 2
    return rounds


def gathered_sum(part, axis):
    total = part.astype(jnp.float32)
    for partner in pairings(lax.axis_size(axis)):
        route = [(i, partner[i]) for i in range(len(partner))]
        total = total + lax.ppermute(total, axis, route)
    return total


def doc_index(positions, doc_ends):
    counted = jnp.sum((positions[:, None] >= doc_ends[None, :]).astype(jnp.int32), axis=1)
    return jnp.where(positions < 0, -1, counted)


def attention_kernel(q_ref, k_ref, v_ref, do_ref, qdoc_ref, kdoc_ref,
                     o_ref, dq_ref, dk_ref, dv_ref, dk_acc, dv_acc):
    qb = pl.program_id(1)
    rows = q_ref.shape[0]
    span = rows + WIN
    key_first = pl.multiple_of(qb * rows, rows)

    @pl.when(qb == 0)
    def _():
        dk_acc[...] = jnp.zeros_like(dk_acc)
        dv_acc[...] = jnp.zeros_like(dv_acc)

    q = jnp.concatenate([q_ref[:, :HEAD_SIZE], q_ref[:, HEAD_SIZE:]], axis=0)
    do = jnp.concatenate([do_ref[:, :HEAD_SIZE], do_ref[:, HEAD_SIZE:]], axis=0)
    k = k_ref[pl.ds(key_first, span), :]
    v = v_ref[pl.ds(key_first, span), :]
    qdoc = qdoc_ref[...]
    qdoc = jnp.concatenate([qdoc, qdoc], axis=0)
    kdoc = kdoc_ref[:, pl.ds(key_first, span)]
    row = lax.broadcasted_iota(jnp.int32, (2 * rows, span), 0) % rows
    col = lax.broadcasted_iota(jnp.int32, (2 * rows, span), 1)
    offset = row + WIN - col
    live = (offset >= 0) & (offset < WIN) & (qdoc == kdoc)

    s = lax.dot_general(q, k, (((1,), (1,)), ((), ())),
                        preferred_element_type=jnp.float32) * softmax_scale
    masked = jnp.where(live, s, masked_value)
    row_max = jnp.max(masked, axis=1, keepdims=True)
    e = jnp.exp(masked - row_max)
    row_sum = jnp.sum(e, axis=1, keepdims=True)
    p = e * (1.0 / row_sum)
    p_low = p.astype(jnp.bfloat16)
    o = jnp.dot(p_low, v, preferred_element_type=jnp.float32)
    row_dot = jnp.sum(do.astype(jnp.float32) * o, axis=1, keepdims=True)
    dp = lax.dot_general(do, v, (((1,), (1,)), ((), ())),
                         preferred_element_type=jnp.float32)
    ds = (p * (dp - row_dot)).astype(jnp.bfloat16)
    dq = jnp.dot(ds, k, preferred_element_type=jnp.float32) * softmax_scale
    dk = jnp.dot(q.T, ds, preferred_element_type=jnp.float32) * softmax_scale
    dv = jnp.dot(do.T, p_low, preferred_element_type=jnp.float32)
    o_ref[:, :HEAD_SIZE] = o[:rows].astype(o_ref.dtype)
    o_ref[:, HEAD_SIZE:] = o[rows:].astype(o_ref.dtype)
    dq_ref[:, :HEAD_SIZE] = dq[:rows].astype(dq_ref.dtype)
    dq_ref[:, HEAD_SIZE:] = dq[rows:].astype(dq_ref.dtype)
    dk_acc[:, pl.ds(key_first, span)] += dk
    dv_acc[:, pl.ds(key_first, span)] += dv

    @pl.when(qb == pl.num_programs(1) - 1)
    def _():
        dk_ref[...] = dk_acc[...].T
        dv_ref[...] = dv_acc[...].T


def fused_attention(queries, extended, output_gradient, qdoc, kdoc, rows=2 * BLK):
    tokens, query_cols = queries.shape
    ext_rows, joined_cols = extended.shape
    groups = joined_cols // (2 * HEAD_SIZE)
    blocks = tokens // rows
    span = rows + WIN
    pair = 2 * HEAD_SIZE
    flops = groups * blocks * 6 * 2 * (2 * rows) * span * HEAD_SIZE
    nbytes = 2 * (4 * tokens * query_cols + ext_rows * joined_cols) + 4 * ext_rows * joined_cols
    return pl.pallas_call(
        attention_kernel,
        grid=(groups, blocks),
        in_specs=[
            pl.BlockSpec((rows, pair), lambda g, b: (b, g)),
            pl.BlockSpec((ext_rows, HEAD_SIZE), lambda g, b: (0, g)),
            pl.BlockSpec((ext_rows, HEAD_SIZE), lambda g, b: (0, g + groups)),
            pl.BlockSpec((rows, pair), lambda g, b: (b, g)),
            pl.BlockSpec((rows, 1), lambda g, b: (b, 0)),
            pl.BlockSpec((1, ext_rows), lambda g, b: (0, 0)),
        ],
        out_specs=[
            pl.BlockSpec((rows, pair), lambda g, b: (b, g)),
            pl.BlockSpec((rows, pair), lambda g, b: (b, g)),
            pl.BlockSpec((ext_rows, HEAD_SIZE), lambda g, b: (0, g)),
            pl.BlockSpec((ext_rows, HEAD_SIZE), lambda g, b: (0, g)),
        ],
        out_shape=[
            jax.ShapeDtypeStruct((tokens, query_cols), jnp.bfloat16),
            jax.ShapeDtypeStruct((tokens, query_cols), jnp.bfloat16),
            jax.ShapeDtypeStruct((ext_rows, joined_cols // 2), jnp.float32),
            jax.ShapeDtypeStruct((ext_rows, joined_cols // 2), jnp.float32),
        ],
        scratch_shapes=[
            pltpu.VMEM((HEAD_SIZE, ext_rows), jnp.float32),
            pltpu.VMEM((HEAD_SIZE, ext_rows), jnp.float32),
        ],
        compiler_params=pltpu.CompilerParams(
            dimension_semantics=("arbitrary", "arbitrary"),
            vmem_limit_bytes=48 * 1024 * 1024,
        ),
        cost_estimate=pl.CostEstimate(
            flops=flops, transcendentals=groups * blocks * 2 * rows * span,
            bytes_accessed=nbytes),
    )(queries, extended, extended, output_gradient, qdoc, kdoc)


def body(
    queries,
    key_head_tensor,
    value_head_tensor,
    output_gradient,
    adapter_up_matrix,
    document_block_counts,
):
    tokens_here = queries.shape[0]
    query_cols = queries.shape[1]
    key_cols = key_head_tensor.shape[1]
    edge_rows = min(WIN, tokens_here)
    hop_count = WIN // edge_rows
    first_pos = lax.axis_index("ctx") * tokens_here
    lowest = first_pos - WIN
    doc_ends = jnp.cumsum(document_block_counts) * BLK
    joined = jnp.concatenate([key_head_tensor, value_head_tensor], axis=1)
    arrived = []
    for hop_num in range(hop_count):
        arrived.append(passed_along(joined, "ctx", hop_num + 1))
    extended = jnp.concatenate(arrived[::-1] + [joined], axis=0)
    qdoc = doc_index(first_pos + jnp.arange(tokens_here, dtype=jnp.int32), doc_ends)
    kdoc = doc_index(lowest + jnp.arange(WIN + tokens_here, dtype=jnp.int32), doc_ends)
    attended, flattened_query, key_grads, value_grads = fused_attention(
        queries, extended, output_gradient, qdoc[:, None], kdoc[None, :]
    )
    halo_grads = jnp.concatenate([key_grads[:WIN], value_grads[:WIN]], axis=1)
    returned = jnp.zeros((edge_rows, 2 * key_cols), jnp.float32)
    for hop_num in range(hop_count):
        segment = halo_grads[
            (hop_count - 1 - hop_num) * edge_rows : (hop_count - hop_num) * edge_rows
        ]
        returned = returned + passed_along(
            segment.astype(jnp.bfloat16), "ctx", -(hop_num + 1)
        ).astype(segment.dtype)
    cut_row = tokens_here - edge_rows
    own = jnp.concatenate([key_grads[WIN:], value_grads[WIN:]], axis=1)
    total = jnp.concatenate([own[:cut_row], own[cut_row:] + returned], axis=0)
    key_total = total[:, :key_cols]
    value_total = total[:, key_cols:]
    adapter_portion = lax.dot_general(
        flattened_query,
        adapter_up_matrix,
        (((1,), (1,)), ((), ())),
        preferred_element_type=jnp.float32,
    )
    adapter_gradient = gathered_sum(adapter_portion, "head")
    return (
        attended,
        flattened_query,
        key_total.astype(jnp.bfloat16),
        value_total.astype(jnp.bfloat16),
        adapter_gradient,
    )


def solution(mesh):
    in_specs = (
        P("ctx", "head"),
        P("ctx", "head"),
        P("ctx", "head"),
        P("ctx", "head"),
        P(None, "head"),
        P(),
    )
    out_specs = (
        P("ctx", "head"),
        P("ctx", "head"),
        P("ctx", "head"),
        P("ctx", "head"),
        P("ctx", None),
    )
    return jax.shard_map(body, mesh=mesh, in_specs=in_specs, out_specs=out_specs, check_vma=False)
```

```python
import functools

import jax
import jax.numpy as jnp
from jax import lax
from jax.experimental import pallas as pl
from jax.experimental.pallas import tpu as pltpu
from jax.sharding import PartitionSpec as P

HEAD_SIZE = 128
WIN = 1024
BLK = 128


softmax_scale = 168.0 ** (-0.5)
masked_value = -1e30


def passed_along(block, axis, distance):
    devices = range(lax.axis_size(axis))
    route = [(i - distance, i) for i in devices if i - distance in devices]
    return lax.ppermute(block, axis, route)


def pairings(count):
    if count == 8:
        return [[i ^ 2 for i in range(8)], [(6 - i) % 8 if i % 2 == 0 else (8 - i) % 8 for i in range(8)], [i ^ 1 for i in range(8)]]
    rounds = []
    stride = 1
    while stride < count:
        rounds.append([i ^ stride for i in range(count)])
        stride *= 2
    return rounds


def gathered_sum(part, axis):
    total = part.astype(jnp.float32)
    for partner in pairings(lax.axis_size(axis)):
        route = [(i, partner[i]) for i in range(len(partner))]
        total = total + lax.ppermute(total, axis, route)
    return total


def doc_index(positions, doc_ends):
    counted = jnp.sum((positions[:, None] >= doc_ends[None, :]).astype(jnp.int32), axis=1)
    return jnp.where(positions < 0, -1, counted)


SPAN_BUCKETS = (2, 4)


def attention_kernel(need_ref, q_ref, k_ref, v_ref, do_ref, qdoc_ref, kdoc_ref,
                     o_ref, dq_ref, dk_ref, dv_ref, dk_acc, dv_acc):
    qb = pl.program_id(1)
    rows = q_ref.shape[0]
    full = (rows + WIN) // rows

    @pl.when(qb == 0)
    def _():
        dk_acc[...] = jnp.zeros_like(dk_acc)
        dv_acc[...] = jnp.zeros_like(dv_acc)

    q = jnp.concatenate([q_ref[:, :HEAD_SIZE], q_ref[:, HEAD_SIZE:]], axis=0)
    do = jnp.concatenate([do_ref[:, :HEAD_SIZE], do_ref[:, HEAD_SIZE:]], axis=0)
    qdoc = qdoc_ref[...]
    qdoc = jnp.concatenate([qdoc, qdoc], axis=0)
    need = need_ref[qb]

    def run(width):
        span = width * rows
        key_first = pl.multiple_of((qb + full - width) * rows, rows)
        k = k_ref[pl.ds(key_first, span), :]
        v = v_ref[pl.ds(key_first, span), :]
        kdoc = kdoc_ref[:, pl.ds(key_first, span)]
        row = lax.broadcasted_iota(jnp.int32, (2 * rows, span), 0) % rows
        col = lax.broadcasted_iota(jnp.int32, (2 * rows, span), 1)
        offset = row + span - rows - col
        live = (offset >= 0) & (offset < WIN) & (qdoc == kdoc)

        s = lax.dot_general(q, k, (((1,), (1,)), ((), ())),
                            preferred_element_type=jnp.float32) * softmax_scale
        masked = jnp.where(live, s, masked_value)
        row_max = jnp.max(masked, axis=1, keepdims=True)
        e = jnp.exp(masked - row_max)
        row_sum = jnp.sum(e, axis=1, keepdims=True)
        p = e * (1.0 / row_sum)
        p_low = p.astype(jnp.bfloat16)
        o = jnp.dot(p_low, v, preferred_element_type=jnp.float32)
        row_dot = jnp.sum(do.astype(jnp.float32) * o, axis=1, keepdims=True)
        dp = lax.dot_general(do, v, (((1,), (1,)), ((), ())),
                             preferred_element_type=jnp.float32)
        ds = (p * (dp - row_dot)).astype(jnp.bfloat16)
        dq = jnp.dot(ds, k, preferred_element_type=jnp.float32) * softmax_scale
        dk = jnp.dot(q.T, ds, preferred_element_type=jnp.float32) * softmax_scale
        dv = jnp.dot(do.T, p_low, preferred_element_type=jnp.float32)
        o_ref[:, :HEAD_SIZE] = o[:rows].astype(o_ref.dtype)
        o_ref[:, HEAD_SIZE:] = o[rows:].astype(o_ref.dtype)
        dq_ref[:, :HEAD_SIZE] = dq[:rows].astype(dq_ref.dtype)
        dq_ref[:, HEAD_SIZE:] = dq[rows:].astype(dq_ref.dtype)
        dk_acc[:, pl.ds(key_first, span)] += dk
        dv_acc[:, pl.ds(key_first, span)] += dv

    low = 0
    for width in SPAN_BUCKETS + (full,):
        pl.when((need > low) & (need <= width))(functools.partial(run, width))
        low = width

    @pl.when(qb == pl.num_programs(1) - 1)
    def _():
        dk_ref[...] = dk_acc[...].T
        dv_ref[...] = dv_acc[...].T


def fused_attention(need, queries, extended, output_gradient, qdoc, kdoc, rows=BLK):
    tokens, query_cols = queries.shape
    ext_rows, joined_cols = extended.shape
    groups = joined_cols // (2 * HEAD_SIZE)
    blocks = tokens // rows
    span = rows + WIN
    pair = 2 * HEAD_SIZE
    flops = groups * blocks * 6 * 2 * (2 * rows) * span * HEAD_SIZE
    nbytes = 2 * (4 * tokens * query_cols + ext_rows * joined_cols) + 4 * ext_rows * joined_cols
    return pl.pallas_call(
        attention_kernel,
        grid=(groups, blocks),
        in_specs=[
            pl.BlockSpec(memory_space=pltpu.SMEM),
            pl.BlockSpec((rows, pair), lambda g, b: (b, g)),
            pl.BlockSpec((ext_rows, HEAD_SIZE), lambda g, b: (0, g)),
            pl.BlockSpec((ext_rows, HEAD_SIZE), lambda g, b: (0, g + groups)),
            pl.BlockSpec((rows, pair), lambda g, b: (b, g)),
            pl.BlockSpec((rows, 1), lambda g, b: (b, 0)),
            pl.BlockSpec((1, ext_rows), lambda g, b: (0, 0)),
        ],
        out_specs=[
            pl.BlockSpec((rows, pair), lambda g, b: (b, g)),
            pl.BlockSpec((rows, pair), lambda g, b: (b, g)),
            pl.BlockSpec((ext_rows, HEAD_SIZE), lambda g, b: (0, g)),
            pl.BlockSpec((ext_rows, HEAD_SIZE), lambda g, b: (0, g)),
        ],
        out_shape=[
            jax.ShapeDtypeStruct((tokens, query_cols), jnp.bfloat16),
            jax.ShapeDtypeStruct((tokens, query_cols), jnp.bfloat16),
            jax.ShapeDtypeStruct((ext_rows, joined_cols // 2), jnp.float32),
            jax.ShapeDtypeStruct((ext_rows, joined_cols // 2), jnp.float32),
        ],
        scratch_shapes=[
            pltpu.VMEM((HEAD_SIZE, ext_rows), jnp.float32),
            pltpu.VMEM((HEAD_SIZE, ext_rows), jnp.float32),
        ],
        compiler_params=pltpu.CompilerParams(
            dimension_semantics=("arbitrary", "arbitrary"),
            vmem_limit_bytes=48 * 1024 * 1024,
        ),
        cost_estimate=pl.CostEstimate(
            flops=flops, transcendentals=groups * blocks * 2 * rows * span,
            bytes_accessed=nbytes),
    )(need, queries, extended, extended, output_gradient, qdoc, kdoc)


def live_key_blocks(block_first, blocks, doc_ends):
    full = (BLK + WIN) // BLK
    local = jnp.arange(blocks, dtype=jnp.int32)
    first_row = (block_first + local) * BLK
    doc = jnp.sum((first_row[:, None] >= doc_ends[None, :]).astype(jnp.int32), axis=1)
    ends = jnp.concatenate([jnp.zeros((1,), jnp.int32), doc_ends.astype(jnp.int32)])
    doc_first = ends[doc] // BLK
    ext_first = doc_first - (block_first - WIN // BLK)
    return jnp.clip(local + full - jnp.maximum(local, ext_first), 1, full).astype(jnp.int32)


def body(
    queries,
    key_head_tensor,
    value_head_tensor,
    output_gradient,
    adapter_up_matrix,
    document_block_counts,
):
    tokens_here = queries.shape[0]
    query_cols = queries.shape[1]
    key_cols = key_head_tensor.shape[1]
    edge_rows = min(WIN, tokens_here)
    hop_count = WIN // edge_rows
    first_pos = lax.axis_index("ctx") * tokens_here
    lowest = first_pos - WIN
    doc_ends = jnp.cumsum(document_block_counts) * BLK
    joined = jnp.concatenate([key_head_tensor, value_head_tensor], axis=1)
    arrived = []
    for hop_num in range(hop_count):
        arrived.append(passed_along(joined, "ctx", hop_num + 1))
    extended = jnp.concatenate(arrived[::-1] + [joined], axis=0)
    qdoc = doc_index(first_pos + jnp.arange(tokens_here, dtype=jnp.int32), doc_ends)
    kdoc = doc_index(lowest + jnp.arange(WIN + tokens_here, dtype=jnp.int32), doc_ends)
    need = live_key_blocks(first_pos // BLK, tokens_here // BLK, doc_ends)
    attended, flattened_query, key_grads, value_grads = fused_attention(
        need,
        queries, extended, output_gradient, qdoc[:, None], kdoc[None, :]
    )
    halo_grads = jnp.concatenate([key_grads[:WIN], value_grads[:WIN]], axis=1)
    returned = jnp.zeros((edge_rows, 2 * key_cols), jnp.float32)
    for hop_num in range(hop_count):
        segment = halo_grads[
            (hop_count - 1 - hop_num) * edge_rows : (hop_count - hop_num) * edge_rows
        ]
        returned = returned + passed_along(
            segment.astype(jnp.bfloat16), "ctx", -(hop_num + 1)
        ).astype(segment.dtype)
    cut_row = tokens_here - edge_rows
    own = jnp.concatenate([key_grads[WIN:], value_grads[WIN:]], axis=1)
    total = jnp.concatenate([own[:cut_row], own[cut_row:] + returned], axis=0)
    key_total = total[:, :key_cols]
    value_total = total[:, key_cols:]
    adapter_portion = lax.dot_general(
        flattened_query,
        adapter_up_matrix,
        (((1,), (1,)), ((), ())),
        preferred_element_type=jnp.float32,
    )
    adapter_gradient = gathered_sum(adapter_portion, "head")
    return (
        attended,
        flattened_query,
        key_total.astype(jnp.bfloat16),
        value_total.astype(jnp.bfloat16),
        adapter_gradient,
    )


def solution(mesh):
    in_specs = (
        P("ctx", "head"),
        P("ctx", "head"),
        P("ctx", "head"),
        P("ctx", "head"),
        P(None, "head"),
        P(),
    )
    out_specs = (
        P("ctx", "head"),
        P("ctx", "head"),
        P("ctx", "head"),
        P("ctx", "head"),
        P("ctx", None),
    )
    return jax.shard_map(body, mesh=mesh, in_specs=in_specs, out_specs=out_specs, check_vma=False)
```

```python
import jax
import jax.numpy as jnp
from jax import lax
from jax.experimental import pallas as pl
from jax.experimental.pallas import tpu as pltpu
from jax.sharding import PartitionSpec as P

HEAD_SIZE = 128
WIN = 1024
BLK = 128


softmax_scale = 168.0 ** (-0.5)
masked_value = -1e30


def passed_along(block, axis, distance):
    devices = range(lax.axis_size(axis))
    route = [(i - distance, i) for i in devices if i - distance in devices]
    return lax.ppermute(block, axis, route)


def pairings(count):
    if count == 8:
        return [[i ^ 2 for i in range(8)], [(6 - i) % 8 if i % 2 == 0 else (8 - i) % 8 for i in range(8)], [i ^ 1 for i in range(8)]]
    rounds = []
    stride = 1
    while stride < count:
        rounds.append([i ^ stride for i in range(count)])
        stride *= 2
    return rounds


def gathered_sum(part, axis):
    total = part.astype(jnp.float32)
    for partner in pairings(lax.axis_size(axis)):
        route = [(i, partner[i]) for i in range(len(partner))]
        total = total + lax.ppermute(total, axis, route)
    return total


def halo_blocks(joined, axis, hop_count):
    count = lax.axis_size(axis)
    near = passed_along(joined, axis, 1)
    if hop_count != 2 or count % 2:
        return [near] + [passed_along(joined, axis, hop + 1) for hop in range(1, hop_count)]
    far_even = lax.ppermute(joined, axis, [(i - 2, i) for i in range(2, count, 2)])
    far_odd = lax.ppermute(near, axis, [(i, i + 1) for i in range(0, count, 2)])
    even = lax.rem(lax.axis_index(axis), 2) == 0
    return [near, jnp.where(even, far_even, far_odd)]


def doc_index(positions, doc_ends):
    counted = jnp.sum((positions[:, None] >= doc_ends[None, :]).astype(jnp.int32), axis=1)
    return jnp.where(positions < 0, -1, counted)


def attention_kernel(q_ref, k_ref, v_ref, do_ref, qdoc_ref, kdoc_ref, bias_ref,
                     o_ref, dq_ref, dk_ref, dv_ref, dk_acc, dv_acc):
    qb = pl.program_id(1)
    rows = q_ref.shape[0]
    span = rows + WIN
    key_first = pl.multiple_of(qb * rows, rows)

    @pl.when(qb == 0)
    def _():
        dk_acc[...] = jnp.zeros_like(dk_acc)
        dv_acc[...] = jnp.zeros_like(dv_acc)

    q = jnp.concatenate([q_ref[:, :HEAD_SIZE], q_ref[:, HEAD_SIZE:]], axis=0)
    do = jnp.concatenate([do_ref[:, :HEAD_SIZE], do_ref[:, HEAD_SIZE:]], axis=0)
    k = k_ref[pl.ds(key_first, span), :]
    v = v_ref[pl.ds(key_first, span), :]
    qdoc = qdoc_ref[...]
    qdoc = jnp.concatenate([qdoc, qdoc], axis=0)
    kdoc = kdoc_ref[:, pl.ds(key_first, span)]

    s = lax.dot_general(q, k, (((1,), (1,)), ((), ())),
                        preferred_element_type=jnp.float32) * softmax_scale
    masked = jnp.where(qdoc == kdoc, s + bias_ref[...], masked_value)
    row_max = jnp.max(masked, axis=1, keepdims=True)
    e = jnp.exp(masked - row_max)
    row_sum = jnp.sum(e, axis=1, keepdims=True)
    p = e * (1.0 / row_sum)
    p_low = p.astype(jnp.bfloat16)
    o = jnp.dot(p_low, v, preferred_element_type=jnp.float32)
    row_dot = jnp.sum(do.astype(jnp.float32) * o, axis=1, keepdims=True)
    dp = lax.dot_general(do, v, (((1,), (1,)), ((), ())),
                         preferred_element_type=jnp.float32)
    ds = (p * (dp - row_dot)).astype(jnp.bfloat16)
    dq = jnp.dot(ds, k, preferred_element_type=jnp.float32) * softmax_scale
    dk = jnp.dot(q.T, ds, preferred_element_type=jnp.float32) * softmax_scale
    dv = jnp.dot(do.T, p_low, preferred_element_type=jnp.float32)
    o_ref[:, :HEAD_SIZE] = o[:rows].astype(o_ref.dtype)
    o_ref[:, HEAD_SIZE:] = o[rows:].astype(o_ref.dtype)
    dq_ref[:, :HEAD_SIZE] = dq[:rows].astype(dq_ref.dtype)
    dq_ref[:, HEAD_SIZE:] = dq[rows:].astype(dq_ref.dtype)
    dk_acc[:, pl.ds(key_first, span)] += dk
    dv_acc[:, pl.ds(key_first, span)] += dv

    @pl.when(qb == pl.num_programs(1) - 1)
    def _():
        dk_ref[...] = dk_acc[...].T
        dv_ref[...] = dv_acc[...].T


def fused_attention(queries, extended, output_gradient, qdoc, kdoc, rows=2 * BLK):
    tokens, query_cols = queries.shape
    ext_rows, joined_cols = extended.shape
    groups = joined_cols // (2 * HEAD_SIZE)
    blocks = tokens // rows
    span = rows + WIN
    pair = 2 * HEAD_SIZE
    flops = groups * blocks * 6 * 2 * (2 * rows) * span * HEAD_SIZE
    nbytes = 2 * (4 * tokens * query_cols + ext_rows * joined_cols) + 4 * ext_rows * joined_cols
    return pl.pallas_call(
        attention_kernel,
        grid=(groups, blocks),
        in_specs=[
            pl.BlockSpec((rows, pair), lambda g, b: (b, g)),
            pl.BlockSpec((ext_rows, HEAD_SIZE), lambda g, b: (0, g)),
            pl.BlockSpec((ext_rows, HEAD_SIZE), lambda g, b: (0, g + groups)),
            pl.BlockSpec((rows, pair), lambda g, b: (b, g)),
            pl.BlockSpec((rows, 1), lambda g, b: (b, 0)),
            pl.BlockSpec((1, ext_rows), lambda g, b: (0, 0)),
            pl.BlockSpec((2 * rows, span), lambda g, b: (0, 0)),
        ],
        out_specs=[
            pl.BlockSpec((rows, pair), lambda g, b: (b, g)),
            pl.BlockSpec((rows, pair), lambda g, b: (b, g)),
            pl.BlockSpec((ext_rows, HEAD_SIZE), lambda g, b: (0, g)),
            pl.BlockSpec((ext_rows, HEAD_SIZE), lambda g, b: (0, g)),
        ],
        out_shape=[
            jax.ShapeDtypeStruct((tokens, query_cols), jnp.bfloat16),
            jax.ShapeDtypeStruct((tokens, query_cols), jnp.bfloat16),
            jax.ShapeDtypeStruct((ext_rows, joined_cols // 2), jnp.float32),
            jax.ShapeDtypeStruct((ext_rows, joined_cols // 2), jnp.float32),
        ],
        scratch_shapes=[
            pltpu.VMEM((HEAD_SIZE, ext_rows), jnp.float32),
            pltpu.VMEM((HEAD_SIZE, ext_rows), jnp.float32),
        ],
        compiler_params=pltpu.CompilerParams(
            dimension_semantics=("arbitrary", "arbitrary"),
            vmem_limit_bytes=48 * 1024 * 1024,
        ),
        cost_estimate=pl.CostEstimate(
            flops=flops, transcendentals=groups * blocks * 2 * rows * span,
            bytes_accessed=nbytes),
    )(queries, extended, extended, output_gradient, qdoc, kdoc, window_bias(rows))


def window_bias(rows):
    span = rows + WIN
    row = lax.broadcasted_iota(jnp.int32, (2 * rows, span), 0) % rows
    col = lax.broadcasted_iota(jnp.int32, (2 * rows, span), 1)
    offset = row + WIN - col
    inside = (offset >= 0) & (offset < WIN)
    return jnp.where(inside, 0.0, masked_value).astype(jnp.float32)


def body(
    queries,
    key_head_tensor,
    value_head_tensor,
    output_gradient,
    adapter_up_matrix,
    document_block_counts,
):
    tokens_here = queries.shape[0]
    query_cols = queries.shape[1]
    key_cols = key_head_tensor.shape[1]
    edge_rows = min(WIN, tokens_here)
    hop_count = WIN // edge_rows
    first_pos = lax.axis_index("ctx") * tokens_here
    lowest = first_pos - WIN
    doc_ends = jnp.cumsum(document_block_counts) * BLK
    joined = jnp.concatenate([key_head_tensor, value_head_tensor], axis=1)
    arrived = halo_blocks(joined, "ctx", hop_count)
    extended = jnp.concatenate(arrived[::-1] + [joined], axis=0)
    qdoc = doc_index(first_pos + jnp.arange(tokens_here, dtype=jnp.int32), doc_ends)
    kdoc = doc_index(lowest + jnp.arange(WIN + tokens_here, dtype=jnp.int32), doc_ends)
    attended, flattened_query, key_grads, value_grads = fused_attention(
        queries, extended, output_gradient, qdoc[:, None], kdoc[None, :]
    )
    halo_grads = jnp.concatenate([key_grads[:WIN], value_grads[:WIN]], axis=1)
    returned = jnp.zeros((edge_rows, 2 * key_cols), jnp.float32)
    for hop_num in range(hop_count):
        segment = halo_grads[
            (hop_count - 1 - hop_num) * edge_rows : (hop_count - hop_num) * edge_rows
        ]
        returned = returned + passed_along(
            segment.astype(jnp.bfloat16), "ctx", -(hop_num + 1)
        ).astype(segment.dtype)
    cut_row = tokens_here - edge_rows
    own = jnp.concatenate([key_grads[WIN:], value_grads[WIN:]], axis=1)
    total = jnp.concatenate([own[:cut_row], own[cut_row:] + returned], axis=0)
    key_total = total[:, :key_cols]
    value_total = total[:, key_cols:]
    adapter_portion = lax.dot_general(
        flattened_query,
        adapter_up_matrix,
        (((1,), (1,)), ((), ())),
        preferred_element_type=jnp.float32,
    )
    adapter_gradient = gathered_sum(adapter_portion, "head")
    return (
        attended,
        flattened_query,
        key_total.astype(jnp.bfloat16),
        value_total.astype(jnp.bfloat16),
        adapter_gradient,
    )


def solution(mesh):
    in_specs = (
        P("ctx", "head"),
        P("ctx", "head"),
        P("ctx", "head"),
        P("ctx", "head"),
        P(None, "head"),
        P(),
    )
    out_specs = (
        P("ctx", "head"),
        P("ctx", "head"),
        P("ctx", "head"),
        P("ctx", "head"),
        P("ctx", None),
    )
    return jax.shard_map(body, mesh=mesh, in_specs=in_specs, out_specs=out_specs, check_vma=False)
```

```python
import jax
import jax.numpy as jnp
from jax import lax
from jax.experimental import pallas as pl
from jax.experimental.pallas import tpu as pltpu
from jax.sharding import PartitionSpec as P

HEAD_SIZE = 128
WIN = 1024
BLK = 128


softmax_scale = 168.0 ** (-0.5)
masked_value = -1e30


def passed_along(block, axis, distance):
    devices = range(lax.axis_size(axis))
    route = [(i - distance, i) for i in devices if i - distance in devices]
    return lax.ppermute(block, axis, route)


def pairings(count):
    if count == 8:
        return [[i ^ 2 for i in range(8)], [(6 - i) % 8 if i % 2 == 0 else (8 - i) % 8 for i in range(8)], [i ^ 1 for i in range(8)]]
    rounds = []
    stride = 1
    while stride < count:
        rounds.append([i ^ stride for i in range(count)])
        stride *= 2
    return rounds


def gathered_sum(part, axis):
    total = part.astype(jnp.float32)
    for partner in pairings(lax.axis_size(axis)):
        route = [(i, partner[i]) for i in range(len(partner))]
        total = total + lax.ppermute(total, axis, route)
    return total


def halo_blocks(joined, axis, hop_count):
    count = lax.axis_size(axis)
    near = passed_along(joined, axis, 1)
    if hop_count != 2 or count % 2:
        return [near] + [passed_along(joined, axis, hop + 1) for hop in range(1, hop_count)]
    far_even = lax.ppermute(joined, axis, [(i - 2, i) for i in range(2, count, 2)])
    far_odd = lax.ppermute(near, axis, [(i, i + 1) for i in range(0, count, 2)])
    even = lax.rem(lax.axis_index(axis), 2) == 0
    return [near, jnp.where(even, far_even, far_odd)]


def doc_index(positions, doc_ends):
    counted = jnp.sum((positions[:, None] >= doc_ends[None, :]).astype(jnp.int32), axis=1)
    return jnp.where(positions < 0, -1, counted)


def attention_kernel(q_ref, k_ref, v_ref, do_ref, qdoc_ref, kdoc_ref,
                     o_ref, dq_ref, dk_ref, dv_ref, dk_acc, dv_acc):
    qb = pl.program_id(1)
    rows = q_ref.shape[0]
    span = rows + WIN
    key_first = pl.multiple_of(qb * rows, rows)

    @pl.when(qb == 0)
    def _():
        dk_acc[...] = jnp.zeros_like(dk_acc)
        dv_acc[...] = jnp.zeros_like(dv_acc)

    q = jnp.concatenate([q_ref[:, :HEAD_SIZE], q_ref[:, HEAD_SIZE:]], axis=0)
    do = jnp.concatenate([do_ref[:, :HEAD_SIZE], do_ref[:, HEAD_SIZE:]], axis=0)
    k = k_ref[pl.ds(key_first, span), :]
    v = v_ref[pl.ds(key_first, span), :]
    qdoc = qdoc_ref[...]
    qdoc = jnp.concatenate([qdoc, qdoc], axis=0)
    kdoc = kdoc_ref[:, pl.ds(key_first, span)]
    row = lax.broadcasted_iota(jnp.int32, (2 * rows, span), 0) % rows
    col = lax.broadcasted_iota(jnp.int32, (2 * rows, span), 1)
    offset = row + WIN - col
    live = (offset >= 0) & (offset < WIN) & (qdoc == kdoc)

    s = lax.dot_general(q, k, (((1,), (1,)), ((), ())),
                        preferred_element_type=jnp.float32) * softmax_scale
    masked = jnp.where(live, s, masked_value)
    row_max = jnp.max(masked, axis=1, keepdims=True)
    e = jnp.exp(masked - row_max)
    row_sum = jnp.sum(e, axis=1, keepdims=True)
    p = e * (1.0 / row_sum)
    p_low = p.astype(jnp.bfloat16)
    o = jnp.dot(p_low, v, preferred_element_type=jnp.float32)
    row_dot = jnp.sum(do.astype(jnp.float32) * o, axis=1, keepdims=True)
    dp = lax.dot_general(do, v, (((1,), (1,)), ((), ())),
                         preferred_element_type=jnp.float32)
    ds = (p * (dp - row_dot)).astype(jnp.bfloat16)
    dq = jnp.dot(ds, k, preferred_element_type=jnp.float32) * softmax_scale
    dk = jnp.dot(q.T, ds, preferred_element_type=jnp.float32) * softmax_scale
    dv = jnp.dot(do.T, p_low, preferred_element_type=jnp.float32)
    o_ref[:, :HEAD_SIZE] = o[:rows].astype(o_ref.dtype)
    o_ref[:, HEAD_SIZE:] = o[rows:].astype(o_ref.dtype)
    dq_ref[:, :HEAD_SIZE] = dq[:rows].astype(dq_ref.dtype)
    dq_ref[:, HEAD_SIZE:] = dq[rows:].astype(dq_ref.dtype)
    dk_acc[:, pl.ds(key_first, span)] += dk
    dv_acc[:, pl.ds(key_first, span)] += dv

    @pl.when(qb == pl.num_programs(1) - 1)
    def _():
        dk_ref[...] = dk_acc[...].T
        dv_ref[...] = dv_acc[...].T


def fused_attention(queries, extended, output_gradient, qdoc, kdoc, rows=2 * BLK):
    tokens, query_cols = queries.shape
    ext_rows, joined_cols = extended.shape
    groups = joined_cols // (2 * HEAD_SIZE)
    blocks = tokens // rows
    span = rows + WIN
    pair = 2 * HEAD_SIZE
    flops = groups * blocks * 6 * 2 * (2 * rows) * span * HEAD_SIZE
    nbytes = 2 * (4 * tokens * query_cols + ext_rows * joined_cols) + 4 * ext_rows * joined_cols
    return pl.pallas_call(
        attention_kernel,
        grid=(groups, blocks),
        in_specs=[
            pl.BlockSpec((rows, pair), lambda g, b: (b, g)),
            pl.BlockSpec((ext_rows, HEAD_SIZE), lambda g, b: (0, g)),
            pl.BlockSpec((ext_rows, HEAD_SIZE), lambda g, b: (0, g + groups)),
            pl.BlockSpec((rows, pair), lambda g, b: (b, g)),
            pl.BlockSpec((rows, 1), lambda g, b: (b, 0)),
            pl.BlockSpec((1, ext_rows), lambda g, b: (0, 0)),
        ],
        out_specs=[
            pl.BlockSpec((rows, pair), lambda g, b: (b, g)),
            pl.BlockSpec((rows, pair), lambda g, b: (b, g)),
            pl.BlockSpec((ext_rows, HEAD_SIZE), lambda g, b: (0, g)),
            pl.BlockSpec((ext_rows, HEAD_SIZE), lambda g, b: (0, g)),
        ],
        out_shape=[
            jax.ShapeDtypeStruct((tokens, query_cols), jnp.bfloat16),
            jax.ShapeDtypeStruct((tokens, query_cols), jnp.bfloat16),
            jax.ShapeDtypeStruct((ext_rows, joined_cols // 2), jnp.float32),
            jax.ShapeDtypeStruct((ext_rows, joined_cols // 2), jnp.float32),
        ],
        scratch_shapes=[
            pltpu.VMEM((HEAD_SIZE, ext_rows), jnp.float32),
            pltpu.VMEM((HEAD_SIZE, ext_rows), jnp.float32),
        ],
        compiler_params=pltpu.CompilerParams(
            dimension_semantics=("arbitrary", "arbitrary"),
            vmem_limit_bytes=48 * 1024 * 1024,
        ),
        cost_estimate=pl.CostEstimate(
            flops=flops, transcendentals=groups * blocks * 2 * rows * span,
            bytes_accessed=nbytes),
    )(queries, extended, extended, output_gradient, qdoc, kdoc)


def body(
    queries,
    key_head_tensor,
    value_head_tensor,
    output_gradient,
    adapter_up_matrix,
    document_block_counts,
):
    tokens_here = queries.shape[0]
    query_cols = queries.shape[1]
    key_cols = key_head_tensor.shape[1]
    edge_rows = min(WIN, tokens_here)
    hop_count = WIN // edge_rows
    first_pos = lax.axis_index("ctx") * tokens_here
    lowest = first_pos - WIN
    doc_ends = jnp.cumsum(document_block_counts) * BLK
    joined = jnp.concatenate([key_head_tensor, value_head_tensor], axis=1)
    arrived = halo_blocks(joined, "ctx", hop_count)
    extended = jnp.concatenate(arrived[::-1] + [joined], axis=0)
    qdoc = doc_index(first_pos + jnp.arange(tokens_here, dtype=jnp.int32), doc_ends)
    kdoc = doc_index(lowest + jnp.arange(WIN + tokens_here, dtype=jnp.int32), doc_ends)
    attended, flattened_query, key_grads, value_grads = fused_attention(
        queries, extended, output_gradient, qdoc[:, None], kdoc[None, :]
    )
    halo_grads = jnp.concatenate([key_grads[:WIN], value_grads[:WIN]], axis=1)
    returned = jnp.zeros((edge_rows, 2 * key_cols), jnp.float32)
    for hop_num in range(hop_count):
        segment = halo_grads[
            (hop_count - 1 - hop_num) * edge_rows : (hop_count - hop_num) * edge_rows
        ]
        returned = returned + passed_along(
            segment.astype(jnp.bfloat16), "ctx", -(hop_num + 1)
        ).astype(segment.dtype)
    cut_row = tokens_here - edge_rows
    own = jnp.concatenate([key_grads[WIN:], value_grads[WIN:]], axis=1)
    total = jnp.concatenate([own[:cut_row], own[cut_row:] + returned], axis=0)
    key_total = total[:, :key_cols]
    value_total = total[:, key_cols:]
    adapter_portion = lax.dot_general(
        flattened_query,
        adapter_up_matrix,
        (((1,), (1,)), ((), ())),
        preferred_element_type=jnp.float32,
    )
    adapter_gradient = gathered_sum(adapter_portion, "head")
    return (
        attended,
        flattened_query,
        key_total.astype(jnp.bfloat16),
        value_total.astype(jnp.bfloat16),
        adapter_gradient,
    )


def solution(mesh):
    in_specs = (
        P("ctx", "head"),
        P("ctx", "head"),
        P("ctx", "head"),
        P("ctx", "head"),
        P(None, "head"),
        P(),
    )
    out_specs = (
        P("ctx", "head"),
        P("ctx", "head"),
        P("ctx", "head"),
        P("ctx", "head"),
        P("ctx", None),
    )
    return jax.shard_map(body, mesh=mesh, in_specs=in_specs, out_specs=out_specs, check_vma=False)
```

```python
import jax
import jax.numpy as jnp
from jax import lax
from jax.experimental import pallas as pl
from jax.experimental.pallas import tpu as pltpu
from jax.sharding import PartitionSpec as P

HEAD_SIZE = 128
WIN = 1024
BLK = 128


softmax_scale = 168.0 ** (-0.5)
masked_value = -1e30


def passed_along(block, axis, distance):
    devices = range(lax.axis_size(axis))
    route = [(i - distance, i) for i in devices if i - distance in devices]
    return lax.ppermute(block, axis, route)


def pairings(count):
    rounds = []
    stride = 1
    while stride < count:
        rounds.append([i ^ stride for i in range(count)])
        stride *= 2
    return rounds


def gathered_sum(part, axis):
    total = part.astype(jnp.float32)
    for partner in pairings(lax.axis_size(axis)):
        route = [(i, partner[i]) for i in range(len(partner))]
        total = total + lax.ppermute(total, axis, route)
    return total


def halo_blocks(joined, axis, hop_count):
    count = lax.axis_size(axis)
    near = passed_along(joined, axis, 1)
    if hop_count != 2 or count % 2:
        return [near] + [passed_along(joined, axis, hop + 1) for hop in range(1, hop_count)]
    far_even = lax.ppermute(joined, axis, [(i - 2, i) for i in range(2, count, 2)])
    far_odd = lax.ppermute(near, axis, [(i, i + 1) for i in range(0, count, 2)])
    even = lax.rem(lax.axis_index(axis), 2) == 0
    return [near, jnp.where(even, far_even, far_odd)]


def doc_index(positions, doc_ends):
    counted = jnp.sum((positions[:, None] >= doc_ends[None, :]).astype(jnp.int32), axis=1)
    return jnp.where(positions < 0, -1, counted)


def attention_kernel(q_ref, k_ref, v_ref, do_ref, qdoc_ref, kdoc_ref, bias_ref,
                     o_ref, dq_ref, dk_ref, dv_ref, dk_acc, dv_acc):
    qb = pl.program_id(1)
    rows = q_ref.shape[0]
    span = rows + WIN
    key_first = pl.multiple_of(qb * rows, rows)

    @pl.when(qb == 0)
    def _():
        dk_acc[...] = jnp.zeros_like(dk_acc)
        dv_acc[...] = jnp.zeros_like(dv_acc)

    q = jnp.concatenate([q_ref[:, :HEAD_SIZE], q_ref[:, HEAD_SIZE:]], axis=0)
    do = jnp.concatenate([do_ref[:, :HEAD_SIZE], do_ref[:, HEAD_SIZE:]], axis=0)
    k = k_ref[pl.ds(key_first, span), :]
    v = v_ref[pl.ds(key_first, span), :]
    qdoc = qdoc_ref[...]
    qdoc = jnp.concatenate([qdoc, qdoc], axis=0)
    kdoc = kdoc_ref[:, pl.ds(key_first, span)]

    s = lax.dot_general(q, k, (((1,), (1,)), ((), ())),
                        preferred_element_type=jnp.float32) * softmax_scale
    masked = jnp.where(qdoc == kdoc, s + bias_ref[...], masked_value)
    row_max = jnp.max(masked, axis=1, keepdims=True)
    e = jnp.exp(masked - row_max)
    row_sum = jnp.sum(e, axis=1, keepdims=True)
    p = e * (1.0 / row_sum)
    p_low = p.astype(jnp.bfloat16)
    o = jnp.dot(p_low, v, preferred_element_type=jnp.float32)
    row_dot = jnp.sum(do.astype(jnp.float32) * o, axis=1, keepdims=True)
    dp = lax.dot_general(do, v, (((1,), (1,)), ((), ())),
                         preferred_element_type=jnp.float32)
    ds = (p * (dp - row_dot)).astype(jnp.bfloat16)
    dq = jnp.dot(ds, k, preferred_element_type=jnp.float32) * softmax_scale
    dk = jnp.dot(q.T, ds, preferred_element_type=jnp.float32) * softmax_scale
    dv = jnp.dot(do.T, p_low, preferred_element_type=jnp.float32)
    o_ref[:, :HEAD_SIZE] = o[:rows].astype(o_ref.dtype)
    o_ref[:, HEAD_SIZE:] = o[rows:].astype(o_ref.dtype)
    dq_ref[:, :HEAD_SIZE] = dq[:rows].astype(dq_ref.dtype)
    dq_ref[:, HEAD_SIZE:] = dq[rows:].astype(dq_ref.dtype)
    dk_acc[:, pl.ds(key_first, span)] += dk
    dv_acc[:, pl.ds(key_first, span)] += dv

    @pl.when(qb == pl.num_programs(1) - 1)
    def _():
        dk_ref[...] = dk_acc[...].T
        dv_ref[...] = dv_acc[...].T


def fused_attention(queries, extended, output_gradient, qdoc, kdoc, rows=2 * BLK):
    tokens, query_cols = queries.shape
    ext_rows, joined_cols = extended.shape
    groups = joined_cols // (2 * HEAD_SIZE)
    blocks = tokens // rows
    span = rows + WIN
    pair = 2 * HEAD_SIZE
    flops = groups * blocks * 6 * 2 * (2 * rows) * span * HEAD_SIZE
    nbytes = 2 * (4 * tokens * query_cols + ext_rows * joined_cols) + 4 * ext_rows * joined_cols
    return pl.pallas_call(
        attention_kernel,
        grid=(groups, blocks),
        in_specs=[
            pl.BlockSpec((rows, pair), lambda g, b: (b, g)),
            pl.BlockSpec((ext_rows, HEAD_SIZE), lambda g, b: (0, g)),
            pl.BlockSpec((ext_rows, HEAD_SIZE), lambda g, b: (0, g + groups)),
            pl.BlockSpec((rows, pair), lambda g, b: (b, g)),
            pl.BlockSpec((rows, 1), lambda g, b: (b, 0)),
            pl.BlockSpec((1, ext_rows), lambda g, b: (0, 0)),
            pl.BlockSpec((2 * rows, span), lambda g, b: (0, 0)),
        ],
        out_specs=[
            pl.BlockSpec((rows, pair), lambda g, b: (b, g)),
            pl.BlockSpec((rows, pair), lambda g, b: (b, g)),
            pl.BlockSpec((ext_rows, HEAD_SIZE), lambda g, b: (0, g)),
            pl.BlockSpec((ext_rows, HEAD_SIZE), lambda g, b: (0, g)),
        ],
        out_shape=[
            jax.ShapeDtypeStruct((tokens, query_cols), jnp.bfloat16),
            jax.ShapeDtypeStruct((tokens, query_cols), jnp.bfloat16),
            jax.ShapeDtypeStruct((ext_rows, joined_cols // 2), jnp.float32),
            jax.ShapeDtypeStruct((ext_rows, joined_cols // 2), jnp.float32),
        ],
        scratch_shapes=[
            pltpu.VMEM((HEAD_SIZE, ext_rows), jnp.float32),
            pltpu.VMEM((HEAD_SIZE, ext_rows), jnp.float32),
        ],
        compiler_params=pltpu.CompilerParams(
            dimension_semantics=("arbitrary", "arbitrary"),
            vmem_limit_bytes=48 * 1024 * 1024,
        ),
        cost_estimate=pl.CostEstimate(
            flops=flops, transcendentals=groups * blocks * 2 * rows * span,
            bytes_accessed=nbytes),
    )(queries, extended, extended, output_gradient, qdoc, kdoc, window_bias(rows))


def window_bias(rows):
    span = rows + WIN
    row = lax.broadcasted_iota(jnp.int32, (2 * rows, span), 0) % rows
    col = lax.broadcasted_iota(jnp.int32, (2 * rows, span), 1)
    offset = row + WIN - col
    inside = (offset >= 0) & (offset < WIN)
    return jnp.where(inside, 0.0, masked_value).astype(jnp.float32)


def body(
    queries,
    key_head_tensor,
    value_head_tensor,
    output_gradient,
    adapter_up_matrix,
    document_block_counts,
):
    tokens_here = queries.shape[0]
    query_cols = queries.shape[1]
    key_cols = key_head_tensor.shape[1]
    edge_rows = min(WIN, tokens_here)
    hop_count = WIN // edge_rows
    first_pos = lax.axis_index("ctx") * tokens_here
    lowest = first_pos - WIN
    doc_ends = jnp.cumsum(document_block_counts) * BLK
    joined = jnp.concatenate([key_head_tensor, value_head_tensor], axis=1)
    arrived = halo_blocks(joined, "ctx", hop_count)
    extended = jnp.concatenate(arrived[::-1] + [joined], axis=0)
    qdoc = doc_index(first_pos + jnp.arange(tokens_here, dtype=jnp.int32), doc_ends)
    kdoc = doc_index(lowest + jnp.arange(WIN + tokens_here, dtype=jnp.int32), doc_ends)
    attended, flattened_query, key_grads, value_grads = fused_attention(
        queries, extended, output_gradient, qdoc[:, None], kdoc[None, :]
    )
    halo_grads = jnp.concatenate([key_grads[:WIN], value_grads[:WIN]], axis=1)
    returned = jnp.zeros((edge_rows, 2 * key_cols), jnp.float32)
    for hop_num in range(hop_count):
        segment = halo_grads[
            (hop_count - 1 - hop_num) * edge_rows : (hop_count - hop_num) * edge_rows
        ]
        returned = returned + passed_along(
            segment.astype(jnp.bfloat16), "ctx", -(hop_num + 1)
        ).astype(segment.dtype)
    cut_row = tokens_here - edge_rows
    own = jnp.concatenate([key_grads[WIN:], value_grads[WIN:]], axis=1)
    total = jnp.concatenate([own[:cut_row], own[cut_row:] + returned], axis=0)
    key_total = total[:, :key_cols]
    value_total = total[:, key_cols:]
    adapter_portion = lax.dot_general(
        flattened_query,
        adapter_up_matrix,
        (((1,), (1,)), ((), ())),
        preferred_element_type=jnp.float32,
    )
    adapter_gradient = gathered_sum(adapter_portion, "head")
    return (
        attended,
        flattened_query,
        key_total.astype(jnp.bfloat16),
        value_total.astype(jnp.bfloat16),
        adapter_gradient,
    )


def solution(mesh):
    in_specs = (
        P("ctx", "head"),
        P("ctx", "head"),
        P("ctx", "head"),
        P("ctx", "head"),
        P(None, "head"),
        P(),
    )
    out_specs = (
        P("ctx", "head"),
        P("ctx", "head"),
        P("ctx", "head"),
        P("ctx", "head"),
        P("ctx", None),
    )
    return jax.shard_map(body, mesh=mesh, in_specs=in_specs, out_specs=out_specs, check_vma=False)
```

```python
import jax
import jax.numpy as jnp
from jax import lax
from jax.experimental import pallas as pl
from jax.experimental.pallas import tpu as pltpu
from jax.sharding import PartitionSpec as P

HEAD_SIZE = 128
WIN = 1024
BLK = 128


softmax_scale = 168.0 ** (-0.5)
masked_value = -1e30


def passed_along(block, axis, distance):
    devices = range(lax.axis_size(axis))
    route = [(i - distance, i) for i in devices if i - distance in devices]
    return lax.ppermute(block, axis, route)


def pairings(count):
    if count == 8:
        return [[i ^ 2 for i in range(8)], [(6 - i) % 8 if i % 2 == 0 else (8 - i) % 8 for i in range(8)], [i ^ 1 for i in range(8)]]
    rounds = []
    stride = 1
    while stride < count:
        rounds.append([i ^ stride for i in range(count)])
        stride *= 2
    return rounds


def gathered_sum(part, axis):
    total = part.astype(jnp.float32)
    for partner in pairings(lax.axis_size(axis)):
        route = [(i, partner[i]) for i in range(len(partner))]
        total = total + lax.ppermute(total, axis, route)
    return total


def halo_blocks(joined, axis, hop_count):
    count = lax.axis_size(axis)
    near = passed_along(joined, axis, 1)
    if hop_count != 2 or count % 2:
        return [near] + [passed_along(joined, axis, hop + 1) for hop in range(1, hop_count)]
    far_even = lax.ppermute(joined, axis, [(i - 2, i) for i in range(2, count, 2)])
    far_odd = lax.ppermute(near, axis, [(i, i + 1) for i in range(0, count, 2)])
    even = lax.rem(lax.axis_index(axis), 2) == 0
    return [near, jnp.where(even, far_even, far_odd)]


def doc_index(positions, doc_ends):
    counted = jnp.sum((positions[:, None] >= doc_ends[None, :]).astype(jnp.int32), axis=1)
    return jnp.where(positions < 0, -1, counted)


def attention_kernel(q_ref, k_ref, v_ref, do_ref, qdoc_ref, kdoc_ref, bias_ref,
                     o_ref, dq_ref, dk_ref, dv_ref, dk_acc, dv_acc):
    qb = pl.program_id(1)
    rows = q_ref.shape[0]
    span = rows + WIN
    key_first = pl.multiple_of(qb * rows, rows)

    @pl.when(qb == 0)
    def _():
        dk_acc[...] = jnp.zeros_like(dk_acc)
        dv_acc[...] = jnp.zeros_like(dv_acc)

    q = jnp.concatenate([q_ref[:, :HEAD_SIZE], q_ref[:, HEAD_SIZE:]], axis=0)
    do = jnp.concatenate([do_ref[:, :HEAD_SIZE], do_ref[:, HEAD_SIZE:]], axis=0)
    k = k_ref[pl.ds(key_first, span), :]
    v = v_ref[pl.ds(key_first, span), :]
    qdoc = qdoc_ref[...]
    qdoc = jnp.concatenate([qdoc, qdoc], axis=0)
    kdoc = kdoc_ref[:, pl.ds(key_first, span)]

    s = lax.dot_general(q, k, (((1,), (1,)), ((), ())),
                        preferred_element_type=jnp.float32) * softmax_scale
    masked = jnp.where(qdoc == kdoc, s + bias_ref[...], masked_value)
    row_max = jnp.max(masked, axis=1, keepdims=True)
    e = jnp.exp(masked - row_max)
    row_sum = jnp.sum(e, axis=1, keepdims=True)
    p = e * (1.0 / row_sum)
    p_low = p.astype(jnp.bfloat16)
    o = jnp.dot(p_low, v, preferred_element_type=jnp.float32)
    row_dot = jnp.sum(do.astype(jnp.float32) * o, axis=1, keepdims=True)
    dp = lax.dot_general(do, v, (((1,), (1,)), ((), ())),
                         preferred_element_type=jnp.float32)
    ds = (p * (dp - row_dot)).astype(jnp.bfloat16)
    dq = jnp.dot(ds, k, preferred_element_type=jnp.float32) * softmax_scale
    dk = jnp.dot(q.T, ds, preferred_element_type=jnp.float32) * softmax_scale
    dv = jnp.dot(do.T, p_low, preferred_element_type=jnp.float32)
    o_ref[:, :HEAD_SIZE] = o[:rows].astype(o_ref.dtype)
    o_ref[:, HEAD_SIZE:] = o[rows:].astype(o_ref.dtype)
    dq_ref[:, :HEAD_SIZE] = dq[:rows].astype(dq_ref.dtype)
    dq_ref[:, HEAD_SIZE:] = dq[rows:].astype(dq_ref.dtype)
    dk_acc[:, pl.ds(key_first, span)] += dk
    dv_acc[:, pl.ds(key_first, span)] += dv

    @pl.when(qb == pl.num_programs(1) - 1)
    def _():
        dk_ref[...] = dk_acc[...].T
        dv_ref[...] = dv_acc[...].T


def fused_attention(queries, extended, output_gradient, qdoc, kdoc, rows=2 * BLK):
    tokens, query_cols = queries.shape
    ext_rows, joined_cols = extended.shape
    groups = joined_cols // (2 * HEAD_SIZE)
    blocks = tokens // rows
    span = rows + WIN
    pair = 2 * HEAD_SIZE
    flops = groups * blocks * 6 * 2 * (2 * rows) * span * HEAD_SIZE
    nbytes = 2 * (4 * tokens * query_cols + ext_rows * joined_cols) + 4 * ext_rows * joined_cols
    return pl.pallas_call(
        attention_kernel,
        grid=(groups, blocks),
        in_specs=[
            pl.BlockSpec((rows, pair), lambda g, b: (b, g)),
            pl.BlockSpec((ext_rows, HEAD_SIZE), lambda g, b: (0, g)),
            pl.BlockSpec((ext_rows, HEAD_SIZE), lambda g, b: (0, g + groups)),
            pl.BlockSpec((rows, pair), lambda g, b: (b, g)),
            pl.BlockSpec((rows, 1), lambda g, b: (b, 0)),
            pl.BlockSpec((1, ext_rows), lambda g, b: (0, 0)),
            pl.BlockSpec((2 * rows, span), lambda g, b: (0, 0)),
        ],
        out_specs=[
            pl.BlockSpec((rows, pair), lambda g, b: (b, g)),
            pl.BlockSpec((rows, pair), lambda g, b: (b, g)),
            pl.BlockSpec((ext_rows, HEAD_SIZE), lambda g, b: (0, g)),
            pl.BlockSpec((ext_rows, HEAD_SIZE), lambda g, b: (0, g)),
        ],
        out_shape=[
            jax.ShapeDtypeStruct((tokens, query_cols), jnp.bfloat16),
            jax.ShapeDtypeStruct((tokens, query_cols), jnp.bfloat16),
            jax.ShapeDtypeStruct((ext_rows, joined_cols // 2), jnp.float32),
            jax.ShapeDtypeStruct((ext_rows, joined_cols // 2), jnp.float32),
        ],
        scratch_shapes=[
            pltpu.VMEM((HEAD_SIZE, ext_rows), jnp.float32),
            pltpu.VMEM((HEAD_SIZE, ext_rows), jnp.float32),
        ],
        compiler_params=pltpu.CompilerParams(
            dimension_semantics=("arbitrary", "arbitrary"),
            vmem_limit_bytes=62 * 1024 * 1024,
        ),
        cost_estimate=pl.CostEstimate(
            flops=flops, transcendentals=groups * blocks * 2 * rows * span,
            bytes_accessed=nbytes),
    )(queries, extended, extended, output_gradient, qdoc, kdoc, window_bias(rows))


def window_bias(rows):
    span = rows + WIN
    row = lax.broadcasted_iota(jnp.int32, (2 * rows, span), 0) % rows
    col = lax.broadcasted_iota(jnp.int32, (2 * rows, span), 1)
    offset = row + WIN - col
    inside = (offset >= 0) & (offset < WIN)
    return jnp.where(inside, 0.0, masked_value).astype(jnp.float32)


def body(
    queries,
    key_head_tensor,
    value_head_tensor,
    output_gradient,
    adapter_up_matrix,
    document_block_counts,
):
    tokens_here = queries.shape[0]
    query_cols = queries.shape[1]
    key_cols = key_head_tensor.shape[1]
    edge_rows = min(WIN, tokens_here)
    hop_count = WIN // edge_rows
    first_pos = lax.axis_index("ctx") * tokens_here
    lowest = first_pos - WIN
    doc_ends = jnp.cumsum(document_block_counts) * BLK
    joined = jnp.concatenate([key_head_tensor, value_head_tensor], axis=1)
    arrived = halo_blocks(joined, "ctx", hop_count)
    extended = jnp.concatenate(arrived[::-1] + [joined], axis=0)
    qdoc = doc_index(first_pos + jnp.arange(tokens_here, dtype=jnp.int32), doc_ends)
    kdoc = doc_index(lowest + jnp.arange(WIN + tokens_here, dtype=jnp.int32), doc_ends)
    attended, flattened_query, key_grads, value_grads = fused_attention(
        queries, extended, output_gradient, qdoc[:, None], kdoc[None, :]
    )
    halo_grads = jnp.concatenate([key_grads[:WIN], value_grads[:WIN]], axis=1)
    returned = jnp.zeros((edge_rows, 2 * key_cols), jnp.float32)
    for hop_num in range(hop_count):
        segment = halo_grads[
            (hop_count - 1 - hop_num) * edge_rows : (hop_count - hop_num) * edge_rows
        ]
        returned = returned + passed_along(
            segment.astype(jnp.bfloat16), "ctx", -(hop_num + 1)
        ).astype(segment.dtype)
    cut_row = tokens_here - edge_rows
    own = jnp.concatenate([key_grads[WIN:], value_grads[WIN:]], axis=1)
    total = jnp.concatenate([own[:cut_row], own[cut_row:] + returned], axis=0)
    key_total = total[:, :key_cols]
    value_total = total[:, key_cols:]
    adapter_portion = lax.dot_general(
        flattened_query,
        adapter_up_matrix,
        (((1,), (1,)), ((), ())),
        preferred_element_type=jnp.float32,
    )
    adapter_gradient = gathered_sum(adapter_portion, "head")
    return (
        attended,
        flattened_query,
        key_total.astype(jnp.bfloat16),
        value_total.astype(jnp.bfloat16),
        adapter_gradient,
    )


def solution(mesh):
    in_specs = (
        P("ctx", "head"),
        P("ctx", "head"),
        P("ctx", "head"),
        P("ctx", "head"),
        P(None, "head"),
        P(),
    )
    out_specs = (
        P("ctx", "head"),
        P("ctx", "head"),
        P("ctx", "head"),
        P("ctx", "head"),
        P("ctx", None),
    )
    return jax.shard_map(body, mesh=mesh, in_specs=in_specs, out_specs=out_specs, check_vma=False)
```
